128 devices in a mesh: wide: 16 (over x, z), narrow: 8 (over y, core).
Axes of the slice: x: 4, y: 4, z: 4, core: 2. Of those that a mesh axis runs over, the one named last changes fastest.
Arguments:
- tokens: bfloat16 [16384, 2048], P(('wide', 'narrow')), may hold values from -6 to 6
- queries: bfloat16 [16384, 2048], P(('wide', 'narrow')), may hold values from -5 to 5
- new_kv: bfloat16 [16384, 1024], P(('wide', 'narrow')), may hold values from -5 to 5
- page_pool: bfloat16 [2048, 64, 1024], P('wide', 'narrow'), may hold values from -5 to 5
- seg_ids: int32 [16, 1024], P('wide'), may hold values from 0 to 15, never falling along the last dimension, each value on 1 to 512 neighbouring positions
- cache_len: int32 [16, 16], P('wide'), may hold values from 64 to 512
- page_table: int32 [16, 16, 8], P('wide'), may hold values from 0 to 7, each once within a row
- moves: int32 [16], replicated, may hold values from 0 to 15, as said below
- out_weight: bfloat16 [2048, 2048], replicated, may hold values from -0.125 to 0.125
- norm_gain: float32 [2048], replicated, may hold values from 0.1 to 1.9
- expert_ids: int32 [16384, 6], P(('wide', 'narrow')), may hold values from 0 to 63, all different within a row; in each aligned block of 128 rows (0 to 127, 128 to 255, ...) at most 16 rows name the same one
- gate_weights: float32 [16384, 6], P(('wide', 'narrow')), may hold values from 0.05 to 0.35
- expert_in: bfloat16 [128, 2048, 1408], P(('wide', 'narrow')), may hold values from -0.125 to 0.125
- expert_out: bfloat16 [128, 704, 2048], P(('wide', 'narrow')), may hold values from -0.15625 to 0.15625
Outputs:
- layer_out: bfloat16 [16384, 2048], P(('wide', 'narrow'))
The draws below stay inside these ranges and needn't reach their ends.
Inputs may be any that keep to these rules, and one draw needn't show every extreme that they name: Slot r of group g holds the request that slot r of group (g - moves[r]) mod 16 held before. No value appears more than 2 times, and some value appears exactly 2 times. The values 1, 15 and 8 each appear. `expert_ids`: within the 128 rows of one device no expert is named more than 16 times; in every draw some device names some expert exactly 16 times. `seg_ids`: never falling along a group's tokens; each of the 16 slots has one token or more. `page_table`: each row is a permutation.
All inputs are finite; a program needn't handle non-finite values.
Results may differ from the reference program's by a relative error of at most 0.006.
Values may be sent and summed in bfloat16 or wider, within the bound.
No kernel may reach another device: no remote copies, remote signals or barrier semaphores. Data moves between devices by JAX's collectives and lax.ppermute only.
A program may use at most 192 MiB of HBM per device.

```python
import math
import jax
import jax.numpy as jnp
import numpy as np
from jax import lax

D = 2048
QH = 16
KVH = 4
HD = 128
FF_E = 1408
TOPK = 6
TOK_DEV = 128
REQS = 16
PAGES_REQ = 8
PAGE = 64
EXPERTS = 64
CAP = 16
GROUP_TOK = 1024
TOKENS = 16384
CACHE_MAX = 512
SEG_MOST = 512
N_WIDE = 16


def draw_queries(key, part):
    own_key = jax.random.fold_in(key, 1)
    values = jnp.clip(jax.random.normal(own_key, (TOKENS, QH * HD), jnp.float32), -5.0, 5.0)
    return values.astype(jnp.bfloat16)


def draw_new_kv(key, part):
    own_key = jax.random.fold_in(key, 2)
    values = jnp.clip(jax.random.normal(own_key, (TOKENS, KVH * 2 * HD), jnp.float32), -5.0, 5.0)
    return values.astype(jnp.bfloat16)


def draw_moves(key, part):
    shuffled = jax.random.permutation(jax.random.fold_in(key, 11), N_WIDE).astype(jnp.int32)
    middle = N_WIDE // 2
    seats = jnp.arange(N_WIDE, dtype=jnp.int32) + 3
    scores = jnp.where(shuffled == middle, 0, jnp.where(shuffled == 1, 1, jnp.where(shuffled == N_WIDE - 1, 2, seats)))
    order = shuffled[jnp.argsort(scores, stable=True)]
    doubled = jnp.concatenate([order, order])
    first = doubled[:REQS]
    final_value = jnp.where(REQS <= N_WIDE, order[0], doubled[REQS - 1])
    first = first.at[REQS - 1].set(final_value)
    shuffle = jax.random.permutation(jax.random.fold_in(key, 12), REQS)
    return first[shuffle].astype(jnp.int32)


def plant(values, stream_key, least, high):
    dims = values.shape
    spot = [jax.random.randint(jax.random.fold_in(stream_key, axis), (), 0, dims[axis]) for axis in range(len(dims))]
    values = values.at[tuple(spot)].set(least)
    longest = dims.index(max(dims))
    spot[longest] = (spot[longest] + 1) % dims[longest]
    return values.at[tuple(spot)].set(high)


def block_scale(key, shape, split, low, top_value):
    level, own = 1.0, jax.random.fold_in(key, 6)
    for dim, blocks in split:
        steps = jnp.exp(jax.random.uniform(jax.random.fold_in(own, dim), (blocks,), jnp.float32, low / len(split), top_value / len(split)))
        level = level * jnp.repeat(steps, shape[dim] // blocks).reshape([-1 if axis == dim else 1 for axis in range(len(shape))])
    return level


def profile(number_of, total, limit, lean):
    weights = [(1 << 20) // math.isqrt(rank ** lean) + 1 for rank in range(2, number_of + 1)]
    spare, counts = total - limit - (number_of - 1), [1] * (number_of - 1)
    while spare > 0:
        free = [i for i in range(number_of - 1) if counts[i] < limit]
        pool, remaining = sum([weights[i] for i in free]), spare
        for i in free:
            more = min(limit - counts[i], max(1, remaining * weights[i] // pool), spare)
            counts[i] = counts[i] + more
            spare = spare - more
    return np.array([limit] + counts)


def ragged_sizes(key, amount, total, limit, slope):
    if amount == 2:
        one = jax.random.randint(key, (), max(1, total - limit), min(limit, total - 1) + 1)
        return jnp.stack([one, total - one])
    tallies = jnp.asarray(profile(amount, total, limit, slope), jnp.int32)
    pairs = (amount - 1) // 2
    donor, sink = tallies[1:1 + 2 * pairs:2], tallies[2:2 + 2 * pairs:2]
    slack = jnp.minimum(donor - 1, limit - sink)
    passed = jax.random.randint(jax.random.fold_in(key, 1), (pairs,), 0, 1 << 20) % (slack + 1)
    tallies = tallies.at[1:1 + 2 * pairs:2].set(donor - passed).at[2:2 + 2 * pairs:2].set(sink + passed)
    return tallies[jax.random.permutation(jax.random.fold_in(key, 2), amount)]


def shared_out(key, own, number, rows, amount, top, reach, lean):
    sequence = jax.random.permutation(key, amount)
    heavy_load, usual = portions_of(amount, rows * top, reach, lean, True), portions_of(amount, rows * top, reach, lean, False)
    places = jnp.arange(amount)

    def named(tallies, turn):
        used = int((tallies > 0).sum())
        fixed = max(1, used // 4)
        moved = fixed + (places - fixed + turn * (used - fixed)) % max(1, amount - fixed)
        return jnp.zeros((amount,), jnp.int32).at[sequence[jnp.where(places < fixed, places, moved)]].set(jnp.asarray(tallies, jnp.int32))

    tallies = jnp.where(number % 4 == 0, named(heavy_load, number // 4), named(usual, number - number // 4 - 1))
    mixed = jax.random.permutation(jax.random.fold_in(own, 3), amount)
    donor, sink = mixed[0:amount // 2 * 2:2], mixed[1:amount // 2 * 2:2]
    room = jnp.minimum(tallies[donor] - 1, reach - tallies[sink]) // 2
    room = jnp.where((donor == sequence[0]) | (sink == sequence[0]) | (tallies[sink] == 0), 0, jnp.maximum(room, 0))
    moved = jax.random.randint(jax.random.fold_in(own, 4), (amount // 2,), 0, 1 << 20) % (room + 1)
    tallies = tallies.at[donor].add(-moved).at[sink].add(moved)
    members = jnp.searchsorted(jnp.cumsum(tallies), jnp.arange(rows * top), side="right").astype(jnp.int32)
    table = members.reshape(top, rows).T
    table = table[jax.random.permutation(jax.random.fold_in(own, 1), rows)]
    turn = jax.random.randint(jax.random.fold_in(own, 2), (rows, 1), 0, top)
    return jnp.take_along_axis(table, (jnp.arange(top)[None, :] + turn) % top, axis=1)


def portions_of(amount, total, limit, lean, full):
    weights = [(1 << 20) // math.isqrt(rank ** lean) + 1 for rank in range(1, amount + 1)]
    largest = limit if full else min(limit, max(-(-total // amount), total * weights[0] // sum(weights)))
    least = 1 if total - largest >= amount - 1 else 0
    holding, spare = [largest] + [least] * (amount - 1), total - largest - least * (amount - 1)
    while spare > 0:
        movable = [i for i in range(1, amount) if holding[i] < largest] or [i for i in range(1, amount) if holding[i] < limit]
        whole, budget = sum([weights[i] for i in movable]), spare
        for i in movable:
            more = min(limit - holding[i], max(1, budget * weights[i] // whole), spare)
            holding[i] = holding[i] + more
            spare = spare - more
    return np.array(holding)


def bell_draw(key, shape, width, most, split=(), kind=jnp.bfloat16):
    result = width * jax.random.normal(key, shape, jnp.float32)
    if split:
        result = result * block_scale(key, shape, split, -0.22, 0.18)
    return jnp.clip(result, -most, most).astype(kind)


def setup_inputs(seed: int = 0) -> dict:
    key_list = jax.random.split(jax.random.key(seed), 15)
    tokens = bell_draw(key_list[0], (TOKENS, D), 1.0, 6.0, ((0, 128),))
    queries = draw_queries(jax.random.fold_in(key_list[14], 71), 0)
    new_kv = draw_new_kv(jax.random.fold_in(key_list[14], 71), 0)
    page_pool = bell_draw(key_list[3], (N_WIDE * REQS * PAGES_REQ, PAGE, KVH * 2 * HD), 1.0, 5.0, ((0, 16), (1, 8)))
    seg_ids = jax.vmap(lambda own: jnp.searchsorted(jnp.cumsum(ragged_sizes(own, REQS, GROUP_TOK, SEG_MOST, 2)), jnp.arange(GROUP_TOK), side="right"))(jax.random.split(key_list[4], N_WIDE)).reshape((N_WIDE, GROUP_TOK)).astype(jnp.int32)
    cache_len = plant(jax.random.randint(key_list[5], (N_WIDE, REQS), PAGE, CACHE_MAX + 1), jax.random.fold_in(key_list[5], 1), PAGE, CACHE_MAX).astype(jnp.int32)
    page_table = jax.vmap(lambda own: jax.random.permutation(own, PAGES_REQ))(jax.random.split(key_list[6], N_WIDE * REQS)).reshape((N_WIDE, REQS, PAGES_REQ)).astype(jnp.int32)
    moves = draw_moves(jax.random.fold_in(key_list[14], 71), 0)
    out_weight = bell_draw(key_list[8], (QH * HD, D), (QH * HD) ** -0.5, 0.125)
    norm_gain = jnp.clip(1.0 + 0.18 * jax.random.normal(key_list[9], (D,), jnp.float32), 0.1, 1.9)
    expert_ids_keys = jax.random.split(jax.random.fold_in(key_list[10], 1), TOKENS // TOK_DEV)
    expert_ids_turns = jax.random.permutation(jax.random.fold_in(key_list[10], 3), TOKENS // TOK_DEV)
    expert_ids = jax.vmap(lambda own, number: shared_out(jax.random.fold_in(key_list[10], 2), own, number, TOK_DEV, EXPERTS, TOPK, CAP, 2))(expert_ids_keys, expert_ids_turns).reshape((TOKENS, TOPK))
    gate_weights = jnp.clip(0.05 + 0.29999999 * jax.random.uniform(key_list[11], (TOKENS, TOPK), jnp.float32) ** block_scale(key_list[11], (TOKENS, TOPK), ((0, 128),), -0.2, 0.2), 0.05, 0.35)
    expert_in = bell_draw(key_list[12], (2 * EXPERTS, D, FF_E), D ** -0.5, 0.125, ((0, 128),))
    expert_out = bell_draw(key_list[13], (2 * EXPERTS, FF_E // 2, D), FF_E ** -0.5, 0.15625, ((0, 128),))
    return {"tokens": tokens, "queries": queries, "new_kv": new_kv, "page_pool": page_pool, "seg_ids": seg_ids, "cache_len": cache_len, "page_table": page_table, "moves": moves, "out_weight": out_weight, "norm_gain": norm_gain, "expert_ids": expert_ids, "gate_weights": gate_weights, "expert_in": expert_in, "expert_out": expert_out}


norm_eps = 1e-06

def group_attention(item, queries, new_kv, page_pool, seg_ids, cache_len, page_table, moves):
    group = item // KVH
    kv_head = item % KVH
    group_size = QH // KVH
    q_group = lax.dynamic_slice(queries, (group * GROUP_TOK, kv_head * group_size * HD), (GROUP_TOK, group_size * HD))
    q_group = q_group.reshape(GROUP_TOK, group_size, HD)
    kv_group = lax.dynamic_slice(new_kv, (group * GROUP_TOK, kv_head * 2 * HD), (GROUP_TOK, 2 * HD))
    sources = (group - moves) % N_WIDE
    first_page = (sources * REQS + jnp.arange(REQS, dtype=jnp.int32)) * PAGES_REQ
    table_row = lax.dynamic_index_in_dim(page_table, group, 0, keepdims=False)
    page_index = (first_page[:, None] + table_row).reshape(-1).astype(jnp.int32)
    pages = jnp.take(page_pool, page_index, axis=0)
    pages = lax.dynamic_slice_in_dim(pages, kv_head * 2 * HD, 2 * HD, axis=2).reshape(REQS * CACHE_MAX, 2 * HD)
    keys = jnp.concatenate([kv_group[:, :HD], pages[:, :HD]], axis=0)
    values = jnp.concatenate([kv_group[:, HD:], pages[:, HD:]], axis=0)
    segment = lax.dynamic_index_in_dim(seg_ids, group, 0, keepdims=False)
    lengths = lax.dynamic_index_in_dim(cache_len, group, 0, keepdims=False)
    positions = jnp.arange(GROUP_TOK, dtype=jnp.int32)
    fresh_ok = (segment[:, None] == segment[None, :]) & (positions[None, :] <= positions[:, None])
    key_req = jnp.arange(REQS * CACHE_MAX, dtype=jnp.int32) // CACHE_MAX
    key_pos = jnp.arange(REQS * CACHE_MAX, dtype=jnp.int32) % CACHE_MAX
    older_ok = (segment[:, None] == key_req[None, :]) & (key_pos[None, :] < lengths[key_req][None, :])
    allowed = jnp.concatenate([fresh_ok, older_ok], axis=1)
    scores = jnp.einsum('qhd,kd->hqk', q_group.astype(jnp.float32), keys.astype(jnp.float32)) * HD ** (-0.5)
    scores = jnp.where(allowed[None], scores, -jnp.inf)
    row_max = lax.optimization_barrier(jnp.max(scores, axis=-1, keepdims=True))
    expd = jnp.exp(scores - row_max)
    probs = (expd / lax.optimization_barrier(jnp.sum(expd, axis=-1, keepdims=True))).astype(jnp.bfloat16)
    attended = jnp.einsum('hqk,kd->qhd', probs.astype(jnp.float32), values.astype(jnp.float32))
    return attended.astype(jnp.bfloat16).reshape(GROUP_TOK, group_size * HD)

def reference(tokens, queries, new_kv, page_pool, seg_ids, cache_len, page_table, moves, out_weight, norm_gain, expert_ids, gate_weights, expert_in, expert_out):

    def attend_item(item):
        return group_attention(item, queries, new_kv, page_pool, seg_ids, cache_len, page_table, moves)
    items = jnp.arange(N_WIDE * KVH, dtype=jnp.int32)
    outputs = lax.map(attend_item, items)
    attended = outputs.reshape(N_WIDE, KVH, GROUP_TOK, -1).transpose(0, 2, 1, 3).reshape(TOKENS, QH * HD)
    residual = tokens.astype(jnp.float32) + jnp.dot(attended, out_weight, preferred_element_type=jnp.float32)
    scale_row = lax.rsqrt(lax.optimization_barrier(jnp.mean(residual * residual, axis=-1, keepdims=True)) + norm_eps)
    normed = (residual * scale_row * norm_gain).astype(jnp.bfloat16)
    flat_ids = expert_ids.reshape(-1)
    flat_gates = gate_weights.reshape(-1)
    token_of = jnp.arange(TOKENS * TOPK, dtype=jnp.int32) // TOPK
    room = 2 * EXPERTS * CAP
    half_units = FF_E // 2

    def one_expert(running, expert):
        hits = flat_ids == expert
        chosen = jnp.nonzero(hits, size=room, fill_value=0)[0]
        used = jnp.arange(room) < jnp.sum(hits.astype(jnp.int32))
        targets = token_of[chosen]
        gathered = jnp.take(normed, targets, axis=0)
        halves = []
        for which_half in range(2):
            weight_in = lax.dynamic_index_in_dim(expert_in, 2 * expert + which_half, 0, keepdims=False)
            weight_out = lax.dynamic_index_in_dim(expert_out, 2 * expert + which_half, 0, keepdims=False)
            both = jnp.dot(gathered, weight_in, preferred_element_type=jnp.float32)
            hidden = (jax.nn.silu(both[:, :half_units]) * both[:, half_units:]).astype(jnp.bfloat16)
            halves.append(jnp.dot(hidden, weight_out, preferred_element_type=jnp.float32))
        partial_value = (halves[0] + halves[1]).astype(jnp.bfloat16)
        weights = jnp.where(used, flat_gates[chosen], jnp.float32(0.0))
        contrib = partial_value.astype(jnp.float32) * weights[:, None]
        return (running.at[targets].add(contrib), None)
    expert_sum, _ = lax.scan(one_expert, jnp.zeros((TOKENS, D), jnp.float32), jnp.arange(EXPERTS, dtype=jnp.int32))
    return (residual + expert_sum).astype(jnp.bfloat16)
```

```python
import functools

import jax
import jax.numpy as jnp
from jax import lax
from jax.sharding import Mesh
from jax.sharding import PartitionSpec as P

QH = 16
KVH = 4
HD = 128
TOPK = 6
PAGE_CAP = 2
NARROW = ("y", "core")
CHIPS = ("wide", "y")
WN = ("wide", "y", "core")


norm_eps = 1e-06
block_limit = 512


def rank_among_equal(values):
    length = values.shape[0]
    order = jnp.arange(length, dtype=jnp.int32)
    earlier = (values[None, :] == values[:, None]) & (order[None, :] < order[:, None])
    return jnp.sum(earlier.astype(jnp.int32), axis=1)


def block_scores(q_block, keys):
    return jnp.einsum("bhd,kd->hbk", q_block, keys, preferred_element_type=jnp.float32) * HD ** (
        -0.5
    )


def fresh_scores(start_row, q_heads, key_new, seg_all, block_len):
    q_block = lax.dynamic_slice_in_dim(q_heads, start_row, block_len, 0)
    seg_block = lax.dynamic_slice_in_dim(seg_all, start_row, block_len, 0)
    row_pos = start_row + jnp.arange(block_len, dtype=jnp.int32)
    positions = jnp.arange(seg_all.shape[0], dtype=jnp.int32)
    visible = (seg_block[:, None] == seg_all[None, :]) & (positions[None, :] <= row_pos[:, None])
    scores = jnp.where(visible[None], block_scores(q_block, key_new), -jnp.inf)
    return (q_block, seg_block, scores)


def attend_masked(
    start_row,
    q_heads,
    key_new,
    value_new,
    key_cached,
    value_cached,
    seg_all,
    lengths,
    cache_max,
    block_len,
):
    q_block, seg_block, fresh = fresh_scores(start_row, q_heads, key_new, seg_all, block_len)
    key_req = jnp.arange(key_cached.shape[0], dtype=jnp.int32) // cache_max
    key_pos = jnp.arange(key_cached.shape[0], dtype=jnp.int32) % cache_max
    visible = (seg_block[:, None] == key_req[None, :]) & (
        key_pos[None, :] < lengths[key_req][None, :]
    )
    older = jnp.where(visible[None], block_scores(q_block, key_cached), -jnp.inf)
    row_max = jnp.maximum(jnp.max(fresh, axis=-1), jnp.max(older, axis=-1))
    fresh_exp = jnp.exp(fresh - row_max[..., None])
    older_exp = jnp.exp(older - row_max[..., None])
    row_total = jnp.sum(fresh_exp, axis=-1) + jnp.sum(older_exp, axis=-1)
    fresh_w = (fresh_exp / row_total[..., None]).astype(jnp.bfloat16)
    older_w = (older_exp / row_total[..., None]).astype(jnp.bfloat16)
    attended = jnp.einsum("hbk,kd->bhd", fresh_w, value_new, preferred_element_type=jnp.float32)
    attended = attended + jnp.einsum(
        "hbk,kd->bhd", older_w, value_cached, preferred_element_type=jnp.float32
    )
    return attended.astype(jnp.bfloat16).reshape(block_len, -1)


def expert_apply(rows_in, expert_in, expert_out):
    dims_in = rows_in.shape
    flat = rows_in.reshape(-1, dims_in[-1])
    both = jnp.dot(flat, expert_in[0], preferred_element_type=jnp.float32)
    half_units = both.shape[1] // 2
    hidden = (jax.nn.silu(both[:, :half_units]) * both[:, half_units:]).astype(jnp.bfloat16)
    half_out = jnp.dot(hidden, expert_out[0], preferred_element_type=jnp.float32)
    return half_out.reshape(dims_in)


def shards(
    tokens,
    queries,
    new_kv,
    page_pool,
    seg_ids,
    cache_len,
    page_table,
    moves,
    out_weight,
    norm_gain,
    expert_ids,
    gate_weights,
    expert_in,
    expert_out,
):
    n_wide = lax.axis_size("wide")
    n_narrow = lax.axis_size("y") * lax.axis_size("core")
    my_group = lax.axis_index("wide")
    tok_dev, width = tokens.shape
    group_tok = tok_dev * n_narrow
    requests = moves.shape[0]
    page_rows = page_pool.shape[1]
    kv_feat = page_pool.shape[2]
    pages_each = page_pool.shape[0] // requests
    heads_here = QH // n_narrow
    group_size = QH // KVH
    ranks = rank_among_equal(moves)
    offsets = jnp.arange(n_wide, dtype=jnp.int32)
    places = jnp.arange(PAGE_CAP, dtype=jnp.int32)
    slot_hits = (moves[None, None, :] == offsets[:, None, None]) & (
        ranks[None, None, :] == places[None, :, None]
    )
    picked = jnp.sum(slot_hits.astype(jnp.int32) * jnp.arange(requests, dtype=jnp.int32), axis=2)
    filled = jnp.any(slot_hits, axis=2)
    by_dest = (offsets - my_group) % n_wide
    picked = picked[by_dest]
    filled = filled[by_dest]
    blocks = page_pool.reshape(requests, pages_each * page_rows, kv_feat)
    outgoing = jnp.take(blocks, picked.reshape(-1), axis=0).reshape(
        n_wide, PAGE_CAP, pages_each * page_rows, kv_feat
    )
    outgoing = jnp.where(filled[:, :, None, None], outgoing, jnp.zeros((), outgoing.dtype))
    arrived = lax.all_to_all(outgoing, "wide", split_axis=0, concat_axis=0, tiled=True)
    sources = (my_group - moves) % n_wide
    first_page = (sources * PAGE_CAP + ranks) * pages_each
    page_index = (first_page[:, None] + page_table[0]).reshape(-1)
    arrived = arrived.reshape(n_wide * PAGE_CAP * pages_each, page_rows, kv_feat)
    cached = jnp.take(arrived, page_index, axis=0)
    kv_of_dest = jnp.arange(n_narrow, dtype=jnp.int32) * heads_here // group_size
    q_send = queries.reshape(1, tok_dev, n_narrow, heads_here * HD)
    kv_send = jnp.take(new_kv.reshape(tok_dev, KVH, 2 * HD), kv_of_dest, axis=1).reshape(
        1, tok_dev, n_narrow, 2 * HD
    )
    cache_send = jnp.take(
        cached.reshape(requests * pages_each, page_rows, KVH, 2 * HD), kv_of_dest, axis=2
    )
    q_heads, kv_heads, cache_heads = (
        lax.all_to_all(q_send, NARROW, split_axis=2, concat_axis=1, tiled=True),
        lax.all_to_all(kv_send, NARROW, split_axis=2, concat_axis=1, tiled=True),
        lax.all_to_all(cache_send, NARROW, split_axis=2, concat_axis=1, tiled=True),
    )
    q_heads = q_heads.reshape(group_tok, heads_here, HD)
    kv_heads = kv_heads.reshape(group_tok, 2 * HD)
    cache_max = pages_each * page_rows * n_narrow
    cache_heads = cache_heads.reshape(requests * cache_max, 2 * HD)
    key_new = kv_heads[:, :HD]
    value_new = kv_heads[:, HD:]
    key_cached = cache_heads[:, :HD]
    value_cached = cache_heads[:, HD:]
    seg_all = seg_ids[0]
    lengths = cache_len[0]
    block_len = min(block_limit, group_tok)
    starts = jnp.arange(group_tok // block_len, dtype=jnp.int32) * block_len
    attend_one = functools.partial(
        attend_masked,
        q_heads=q_heads,
        key_new=key_new,
        value_new=value_new,
        key_cached=key_cached,
        value_cached=value_cached,
        seg_all=seg_all,
        lengths=lengths,
        cache_max=cache_max,
        block_len=block_len,
    )
    attended = lax.map(attend_one, starts).reshape(n_narrow, tok_dev, heads_here * HD)
    back_home = lax.all_to_all(attended, NARROW, split_axis=0, concat_axis=2, tiled=True)
    mixed = back_home.reshape(tok_dev, QH * HD)
    residual = tokens.astype(jnp.float32) + jnp.dot(
        mixed, out_weight, preferred_element_type=jnp.float32
    )
    scale_row = lax.rsqrt(jnp.mean(residual * residual, axis=-1, keepdims=True) + norm_eps)
    normed = (residual * scale_row * norm_gain).astype(jnp.bfloat16)
    experts = n_wide * n_narrow // 2
    capacity = tok_dev * TOPK * 4 // (3 * experts)
    flat_ids = expert_ids.reshape(-1)
    onehot = (flat_ids[:, None] == jnp.arange(experts, dtype=jnp.int32)[None, :]).astype(jnp.int32)
    before = jnp.cumsum(onehot, axis=0) - onehot
    slot_place = jnp.sum(before * onehot, axis=1)
    slot_of = flat_ids * capacity + slot_place
    token_of = jnp.arange(tok_dev * TOPK, dtype=jnp.int32) // TOPK
    slot_token = jnp.zeros((experts * capacity,), jnp.int32).at[slot_of].set(token_of)
    slot_used = jnp.zeros((experts * capacity,), jnp.bool_).at[slot_of].set(True)
    outgoing_rows = jnp.where(
        slot_used[:, None], jnp.take(normed, slot_token, axis=0), jnp.zeros((), jnp.bfloat16)
    )
    outgoing_rows = outgoing_rows.reshape(experts, capacity, width)
    at_chip = lax.all_to_all(outgoing_rows, CHIPS, split_axis=0, concat_axis=0, tiled=True)
    both_cores = lax.all_gather(at_chip, "core", axis=0, tiled=False)
    half_out = expert_apply(both_cores, expert_in, expert_out)
    core = lax.axis_index("core")
    mine = lax.dynamic_index_in_dim(half_out, core, 0, keepdims=False)
    theirs = lax.dynamic_index_in_dim(half_out, 1 - core, 0, keepdims=False)
    partner = lax.ppermute(theirs, "core", perm=[(0, 1), (1, 0)])
    summed = (mine + partner).astype(jnp.bfloat16)
    returned = lax.all_to_all(summed, CHIPS, split_axis=0, concat_axis=0, tiled=True)
    summed_rows = returned.reshape(experts * capacity, width)
    picked_rows = jnp.take(summed_rows, slot_of, axis=0)
    weighted = picked_rows.astype(jnp.float32) * gate_weights.reshape(-1)[:, None]
    expert_sum = jnp.sum(weighted.reshape(tok_dev, TOPK, width), axis=1)
    return (residual + expert_sum).astype(jnp.bfloat16)


def solution(mesh):
    placed = (
        P(WN, None),
        P(WN, None),
        P(WN, None),
        P("wide", NARROW, None),
        P("wide", None),
        P("wide", None),
        P("wide", None, None),
        P(),
        P(),
        P(),
        P(WN, None),
        P(WN, None),
        P(WN, None, None),
        P(WN, None, None),
    )
    mesh = Mesh(mesh.devices.reshape(mesh.shape["wide"], -1, 2), ("wide", "y", "core"))
    return jax.shard_map(
        shards, mesh=mesh, in_specs=placed, out_specs=P(WN, None), check_vma=False
    )
```

```python
import functools

import jax
import jax.numpy as jnp
from jax import lax
from jax.experimental import pallas as pl
from jax.experimental.pallas import tpu as pltpu
from jax.sharding import Mesh
from jax.sharding import PartitionSpec as P

QH = 16
KVH = 4
HD = 128
TOPK = 6
PAGE_CAP = 2
NARROW = ("y", "core")
CHIPS = ("wide", "y")
WN = ("wide", "y", "core")


norm_eps = 1e-06
block_limit = 512
BQ = 128
BK = 128
LANES = 128


def rank_among_equal(values):
    length = values.shape[0]
    order = jnp.arange(length, dtype=jnp.int32)
    earlier = (values[None, :] == values[:, None]) & (order[None, :] < order[:, None])
    return jnp.sum(earlier.astype(jnp.int32), axis=1)


def block_scores(q_block, keys):
    return jnp.einsum("bhd,kd->hbk", q_block, keys, preferred_element_type=jnp.float32) * HD ** (
        -0.5
    )


def fresh_scores(start_row, q_heads, key_new, seg_all, block_len):
    q_block = lax.dynamic_slice_in_dim(q_heads, start_row, block_len, 0)
    seg_block = lax.dynamic_slice_in_dim(seg_all, start_row, block_len, 0)
    row_pos = start_row + jnp.arange(block_len, dtype=jnp.int32)
    positions = jnp.arange(seg_all.shape[0], dtype=jnp.int32)
    visible = (seg_block[:, None] == seg_all[None, :]) & (positions[None, :] <= row_pos[:, None])
    scores = jnp.where(visible[None], block_scores(q_block, key_new), -jnp.inf)
    return (q_block, seg_block, scores)


def attend_masked(
    start_row,
    q_heads,
    key_new,
    value_new,
    key_cached,
    value_cached,
    seg_all,
    lengths,
    cache_max,
    block_len,
):
    q_block, seg_block, fresh = fresh_scores(start_row, q_heads, key_new, seg_all, block_len)
    key_req = jnp.arange(key_cached.shape[0], dtype=jnp.int32) // cache_max
    key_pos = jnp.arange(key_cached.shape[0], dtype=jnp.int32) % cache_max
    visible = (seg_block[:, None] == key_req[None, :]) & (
        key_pos[None, :] < lengths[key_req][None, :]
    )
    older = jnp.where(visible[None], block_scores(q_block, key_cached), -jnp.inf)
    row_max = jnp.maximum(jnp.max(fresh, axis=-1), jnp.max(older, axis=-1))
    fresh_exp = jnp.exp(fresh - row_max[..., None])
    older_exp = jnp.exp(older - row_max[..., None])
    row_total = jnp.sum(fresh_exp, axis=-1) + jnp.sum(older_exp, axis=-1)
    fresh_w = (fresh_exp / row_total[..., None]).astype(jnp.bfloat16)
    older_w = (older_exp / row_total[..., None]).astype(jnp.bfloat16)
    attended = jnp.einsum("hbk,kd->bhd", fresh_w, value_new, preferred_element_type=jnp.float32)
    attended = attended + jnp.einsum(
        "hbk,kd->bhd", older_w, value_cached, preferred_element_type=jnp.float32
    )
    return attended.astype(jnp.bfloat16).reshape(block_len, -1)


def slot_attention(q_rows, kv_new, kv_cached, seg_all, lengths, cache_max):
    tokens = q_rows.shape[0]
    slots = lengths.shape[0]
    scale = HD ** (-0.5)
    n_q = tokens // BQ
    new_steps = (cache_max + BQ) // BK
    steps = new_steps + slots
    seg_start = jnp.sum(
        (seg_all[None, :] < jnp.arange(slots, dtype=jnp.int32)[:, None]).astype(jnp.int32), axis=1
    )
    firsts = seg_all[::BQ]
    lasts = seg_all[BQ - 1 :: BQ]
    kb_hi = (jnp.arange(n_q, dtype=jnp.int32) * BQ + BQ - 1) // BK
    kb_lo = jnp.maximum(seg_start[firsts] // BK, kb_hi - (new_steps - 1))
    n_new = kb_hi - kb_lo + 1
    n_old = lasts - firsts + 1
    t = jnp.arange(steps, dtype=jnp.int32)[None, :]
    new_idx = (kb_lo[:, None] + jnp.minimum(t, n_new[:, None] - 1)).reshape(-1)
    old_idx = (firsts[:, None] + jnp.clip(t - n_new[:, None], 0, n_old[:, None] - 1)).reshape(-1)
    counts = jnp.stack([n_new, n_old], axis=1).reshape(-1)
    q2 = q_rows.reshape(n_q, BQ, 2, HD).transpose(0, 2, 1, 3).reshape(n_q, 2 * BQ, HD)
    seg_q = jnp.broadcast_to(seg_all.reshape(n_q, 1, BQ, 1), (n_q, 2, BQ, LANES)).reshape(n_q, 2 * BQ, LANES)
    seg_k = jnp.broadcast_to(seg_all.reshape(tokens // BK, 1, BK), (tokens // BK, 8, BK))
    cached = kv_cached.reshape(slots, cache_max, 2 * HD)

    def kernel(new_sm, old_sm, cnt_sm, len_sm, q_ref, segq_ref, kn_ref, vn_ref, segk_ref, kc_ref, vc_ref, o_ref,
               m_ref, l_ref, acc_ref):
        b = pl.program_id(0)
        t2 = pl.program_id(1)
        second = t2 >= steps
        step = t2 - jnp.where(second, steps, 0)
        nn = cnt_sm[2 * b]
        no = cnt_sm[2 * b + 1]

        @pl.when(t2 == 0)
        def _():
            m_ref[...] = jnp.full(m_ref.shape, -1e30, jnp.float32)
            l_ref[...] = jnp.zeros(l_ref.shape, jnp.float32)
            acc_ref[...] = jnp.zeros(acc_ref.shape, jnp.float32)

        def widen(x, width):
            return x if width == LANES else jnp.concatenate([x] * (width // LANES), axis=1)

        def visit(s, v):
            @pl.when(jnp.logical_not(second))
            def _():
                m = m_ref[...]
                m_new = jnp.maximum(m, jnp.max(s, axis=1, keepdims=True))
                wide_m = widen(m_new, s.shape[1])
                l_ref[...] = l_ref[...] * jnp.exp(m - m_new) + jnp.sum(
                    jnp.exp(s - wide_m), axis=1, keepdims=True)
                m_ref[...] = m_new

            @pl.when(second)
            def _():
                width = s.shape[1]
                p = (jnp.exp(s - widen(m_ref[...], width)) / widen(l_ref[...], width)).astype(jnp.bfloat16)
                acc_ref[...] += jnp.dot(p, v, preferred_element_type=jnp.float32)

        q = q_ref[0]
        sq = segq_ref[0]

        @pl.when(step < nn)
        def _():
            kb = new_sm[b * steps + step]
            s = lax.dot_general(q, kn_ref[...], (((1,), (1,)), ((), ())),
                                preferred_element_type=jnp.float32) * scale
            rows = lax.broadcasted_iota(jnp.int32, s.shape, 0)
            cols = lax.broadcasted_iota(jnp.int32, s.shape, 1)
            qpos = b * BQ + jnp.bitwise_and(rows, BQ - 1)
            vis = (sq == segk_ref[0][:1, :]) & (kb * BK + cols <= qpos)
            visit(jnp.where(vis, s, -jnp.inf), vn_ref[...])

        @pl.when((step >= nn) & (step < nn + no))
        def _():
            r = old_sm[b * steps + step]
            s = lax.dot_general(q, kc_ref[0], (((1,), (1,)), ((), ())),
                                preferred_element_type=jnp.float32) * scale
            cols = lax.broadcasted_iota(jnp.int32, s.shape, 1)
            vis = (widen(sq, s.shape[1]) == r) & (cols < len_sm[r])
            visit(jnp.where(vis, s, -jnp.inf), vc_ref[0])

        @pl.when(t2 == 2 * steps - 1)
        def _():
            o_ref[0] = acc_ref[...].astype(jnp.bfloat16)

    def at(table):
        return lambda b, t2, new_sm, old_sm, cnt_sm, len_sm: table(b, t2 % steps, new_sm, old_sm)

    grid_spec = pltpu.PrefetchScalarGridSpec(
        num_scalar_prefetch=4,
        grid=(n_q, 2 * steps),
        in_specs=[
            pl.BlockSpec((1, 2 * BQ, HD), lambda b, t2, *_: (b, 0, 0)),
            pl.BlockSpec((1, 2 * BQ, LANES), lambda b, t2, *_: (b, 0, 0)),
            pl.BlockSpec((BK, HD), at(lambda b, t, n, o: (n[b * steps + t], 0))),
            pl.BlockSpec((BK, HD), at(lambda b, t, n, o: (n[b * steps + t], 1))),
            pl.BlockSpec((1, 8, BK), at(lambda b, t, n, o: (n[b * steps + t], 0, 0))),
            pl.BlockSpec((1, cache_max, HD), at(lambda b, t, n, o: (o[b * steps + t], 0, 0))),
            pl.BlockSpec((1, cache_max, HD), at(lambda b, t, n, o: (o[b * steps + t], 0, 1))),
        ],
        out_specs=pl.BlockSpec((1, 2 * BQ, HD), lambda b, t2, *_: (b, 0, 0)),
        scratch_shapes=[
            pltpu.VMEM((2 * BQ, LANES), jnp.float32),
            pltpu.VMEM((2 * BQ, LANES), jnp.float32),
            pltpu.VMEM((2 * BQ, HD), jnp.float32),
        ],
    )
    out = pl.pallas_call(
        kernel,
        grid_spec=grid_spec,
        out_shape=jax.ShapeDtypeStruct((n_q, 2 * BQ, HD), jnp.bfloat16),
    )(new_idx, old_idx, counts, lengths, q2, seg_q, kv_new, kv_new, seg_k, cached, cached)
    return out.reshape(n_q, 2, BQ, HD).transpose(0, 2, 1, 3).reshape(tokens, 2 * HD)


def expert_apply(rows_in, expert_in, expert_out):
    dims_in = rows_in.shape
    flat = rows_in.reshape(-1, dims_in[-1])
    both = jnp.dot(flat, expert_in[0], preferred_element_type=jnp.float32)
    half_units = both.shape[1] // 2
    hidden = (jax.nn.silu(both[:, :half_units]) * both[:, half_units:]).astype(jnp.bfloat16)
    half_out = jnp.dot(hidden, expert_out[0], preferred_element_type=jnp.float32)
    return half_out.reshape(dims_in)


def shards(
    tokens,
    queries,
    new_kv,
    page_pool,
    seg_ids,
    cache_len,
    page_table,
    moves,
    out_weight,
    norm_gain,
    expert_ids,
    gate_weights,
    expert_in,
    expert_out,
):
    n_wide = lax.axis_size("wide")
    n_narrow = lax.axis_size("y") * lax.axis_size("core")
    my_group = lax.axis_index("wide")
    tok_dev, width = tokens.shape
    group_tok = tok_dev * n_narrow
    requests = moves.shape[0]
    page_rows = page_pool.shape[1]
    kv_feat = page_pool.shape[2]
    pages_each = page_pool.shape[0] // requests
    heads_here = QH // n_narrow
    group_size = QH // KVH
    ranks = rank_among_equal(moves)
    offsets = jnp.arange(n_wide, dtype=jnp.int32)
    places = jnp.arange(PAGE_CAP, dtype=jnp.int32)
    slot_hits = (moves[None, None, :] == offsets[:, None, None]) & (
        ranks[None, None, :] == places[None, :, None]
    )
    picked = jnp.sum(slot_hits.astype(jnp.int32) * jnp.arange(requests, dtype=jnp.int32), axis=2)
    filled = jnp.any(slot_hits, axis=2)
    by_dest = (offsets - my_group) % n_wide
    picked = picked[by_dest]
    filled = filled[by_dest]
    blocks = page_pool.reshape(requests, pages_each * page_rows, kv_feat)
    outgoing = jnp.take(blocks, picked.reshape(-1), axis=0).reshape(
        n_wide, PAGE_CAP, pages_each * page_rows, kv_feat
    )
    outgoing = jnp.where(filled[:, :, None, None], outgoing, jnp.zeros((), outgoing.dtype))
    arrived = lax.all_to_all(outgoing, "wide", split_axis=0, concat_axis=0, tiled=True)
    sources = (my_group - moves) % n_wide
    first_page = (sources * PAGE_CAP + ranks) * pages_each
    page_index = (first_page[:, None] + page_table[0]).reshape(-1)
    arrived = arrived.reshape(n_wide * PAGE_CAP * pages_each, page_rows, kv_feat)
    cached = jnp.take(arrived, page_index, axis=0)
    kv_of_dest = jnp.arange(n_narrow, dtype=jnp.int32) * heads_here // group_size
    q_send = queries.reshape(1, tok_dev, n_narrow, heads_here * HD)
    kv_send = jnp.take(new_kv.reshape(tok_dev, KVH, 2 * HD), kv_of_dest, axis=1).reshape(
        1, tok_dev, n_narrow, 2 * HD
    )
    cache_send = jnp.take(
        cached.reshape(requests * pages_each, page_rows, KVH, 2 * HD), kv_of_dest, axis=2
    )
    q_heads, kv_heads, cache_heads = (
        lax.all_to_all(q_send, NARROW, split_axis=2, concat_axis=1, tiled=True),
        lax.all_to_all(kv_send, NARROW, split_axis=2, concat_axis=1, tiled=True),
        lax.all_to_all(cache_send, NARROW, split_axis=2, concat_axis=1, tiled=True),
    )
    q_heads = q_heads.reshape(group_tok, heads_here, HD)
    kv_heads = kv_heads.reshape(group_tok, 2 * HD)
    cache_max = pages_each * page_rows * n_narrow
    cache_heads = cache_heads.reshape(requests * cache_max, 2 * HD)
    key_new = kv_heads[:, :HD]
    value_new = kv_heads[:, HD:]
    key_cached = cache_heads[:, :HD]
    value_cached = cache_heads[:, HD:]
    seg_all = seg_ids[0]
    lengths = cache_len[0]
    attended = slot_attention(
        q_heads.reshape(group_tok, heads_here * HD), kv_heads, cache_heads, seg_all, lengths, cache_max
    ).reshape(n_narrow, tok_dev, heads_here * HD)
    back_home = lax.all_to_all(attended, NARROW, split_axis=0, concat_axis=2, tiled=True)
    mixed = back_home.reshape(tok_dev, QH * HD)
    residual = tokens.astype(jnp.float32) + jnp.dot(
        mixed, out_weight, preferred_element_type=jnp.float32
    )
    scale_row = lax.rsqrt(jnp.mean(residual * residual, axis=-1, keepdims=True) + norm_eps)
    normed = (residual * scale_row * norm_gain).astype(jnp.bfloat16)
    experts = n_wide * n_narrow // 2
    capacity = tok_dev * TOPK * 4 // (3 * experts)
    flat_ids = expert_ids.reshape(-1)
    onehot = (flat_ids[:, None] == jnp.arange(experts, dtype=jnp.int32)[None, :]).astype(jnp.int32)
    before = jnp.cumsum(onehot, axis=0) - onehot
    slot_place = jnp.sum(before * onehot, axis=1)
    slot_of = flat_ids * capacity + slot_place
    token_of = jnp.arange(tok_dev * TOPK, dtype=jnp.int32) // TOPK
    slot_token = jnp.zeros((experts * capacity,), jnp.int32).at[slot_of].set(token_of)
    slot_used = jnp.zeros((experts * capacity,), jnp.bool_).at[slot_of].set(True)
    outgoing_rows = jnp.where(
        slot_used[:, None], jnp.take(normed, slot_token, axis=0), jnp.zeros((), jnp.bfloat16)
    )
    outgoing_rows = outgoing_rows.reshape(experts, capacity, width)
    at_chip = lax.all_to_all(outgoing_rows, CHIPS, split_axis=0, concat_axis=0, tiled=True)
    both_cores = lax.all_gather(at_chip, "core", axis=0, tiled=False)
    half_out = expert_apply(both_cores, expert_in, expert_out)
    core = lax.axis_index("core")
    mine = lax.dynamic_index_in_dim(half_out, core, 0, keepdims=False)
    theirs = lax.dynamic_index_in_dim(half_out, 1 - core, 0, keepdims=False)
    partner = lax.ppermute(theirs, "core", perm=[(0, 1), (1, 0)])
    summed = (mine + partner).astype(jnp.bfloat16)
    returned = lax.all_to_all(summed, CHIPS, split_axis=0, concat_axis=0, tiled=True)
    summed_rows = returned.reshape(experts * capacity, width)
    picked_rows = jnp.take(summed_rows, slot_of, axis=0)
    weighted = picked_rows.astype(jnp.float32) * gate_weights.reshape(-1)[:, None]
    expert_sum = jnp.sum(weighted.reshape(tok_dev, TOPK, width), axis=1)
    return (residual + expert_sum).astype(jnp.bfloat16)


def solution(mesh):
    placed = (
        P(WN, None),
        P(WN, None),
        P(WN, None),
        P("wide", NARROW, None),
        P("wide", None),
        P("wide", None),
        P("wide", None, None),
        P(),
        P(),
        P(),
        P(WN, None),
        P(WN, None),
        P(WN, None, None),
        P(WN, None, None),
    )
    mesh = Mesh(mesh.devices.reshape(mesh.shape["wide"], -1, 2), ("wide", "y", "core"))
    return jax.shard_map(
        shards, mesh=mesh, in_specs=placed, out_specs=P(WN, None), check_vma=False
    )
```

```python
import functools

import jax
import jax.numpy as jnp
from jax import lax
from jax.experimental import pallas as pl
from jax.experimental.pallas import tpu as pltpu
from jax.sharding import Mesh
from jax.sharding import PartitionSpec as P

QH = 16
KVH = 4
HD = 128
TOPK = 6
PAGE_CAP = 2
NARROW = ("y", "core")
CHIPS = ("wide", "y")
WN = ("wide", "y", "core")


norm_eps = 1e-06
block_limit = 512
BQ = 128
BK = 128
LANES = 128


def rank_among_equal(values):
    length = values.shape[0]
    order = jnp.arange(length, dtype=jnp.int32)
    earlier = (values[None, :] == values[:, None]) & (order[None, :] < order[:, None])
    return jnp.sum(earlier.astype(jnp.int32), axis=1)


def block_scores(q_block, keys):
    return jnp.einsum("bhd,kd->hbk", q_block, keys, preferred_element_type=jnp.float32) * HD ** (
        -0.5
    )


def fresh_scores(start_row, q_heads, key_new, seg_all, block_len):
    q_block = lax.dynamic_slice_in_dim(q_heads, start_row, block_len, 0)
    seg_block = lax.dynamic_slice_in_dim(seg_all, start_row, block_len, 0)
    row_pos = start_row + jnp.arange(block_len, dtype=jnp.int32)
    positions = jnp.arange(seg_all.shape[0], dtype=jnp.int32)
    visible = (seg_block[:, None] == seg_all[None, :]) & (positions[None, :] <= row_pos[:, None])
    scores = jnp.where(visible[None], block_scores(q_block, key_new), -jnp.inf)
    return (q_block, seg_block, scores)


def attend_masked(
    start_row,
    q_heads,
    key_new,
    value_new,
    key_cached,
    value_cached,
    seg_all,
    lengths,
    cache_max,
    block_len,
):
    q_block, seg_block, fresh = fresh_scores(start_row, q_heads, key_new, seg_all, block_len)
    key_req = jnp.arange(key_cached.shape[0], dtype=jnp.int32) // cache_max
    key_pos = jnp.arange(key_cached.shape[0], dtype=jnp.int32) % cache_max
    visible = (seg_block[:, None] == key_req[None, :]) & (
        key_pos[None, :] < lengths[key_req][None, :]
    )
    older = jnp.where(visible[None], block_scores(q_block, key_cached), -jnp.inf)
    row_max = jnp.maximum(jnp.max(fresh, axis=-1), jnp.max(older, axis=-1))
    fresh_exp = jnp.exp(fresh - row_max[..., None])
    older_exp = jnp.exp(older - row_max[..., None])
    row_total = jnp.sum(fresh_exp, axis=-1) + jnp.sum(older_exp, axis=-1)
    fresh_w = (fresh_exp / row_total[..., None]).astype(jnp.bfloat16)
    older_w = (older_exp / row_total[..., None]).astype(jnp.bfloat16)
    attended = jnp.einsum("hbk,kd->bhd", fresh_w, value_new, preferred_element_type=jnp.float32)
    attended = attended + jnp.einsum(
        "hbk,kd->bhd", older_w, value_cached, preferred_element_type=jnp.float32
    )
    return attended.astype(jnp.bfloat16).reshape(block_len, -1)


def slot_attention(q_rows, kv_new, kv_cached, seg_all, lengths, cache_max):
    tokens = q_rows.shape[0]
    slots = lengths.shape[0]
    scale = HD ** (-0.5)
    n_q = tokens // BQ
    new_steps = (cache_max + BQ) // BK
    steps = new_steps + slots
    seg_start = jnp.sum(
        (seg_all[None, :] < jnp.arange(slots, dtype=jnp.int32)[:, None]).astype(jnp.int32), axis=1
    )
    firsts = seg_all[::BQ]
    lasts = seg_all[BQ - 1 :: BQ]
    kb_hi = (jnp.arange(n_q, dtype=jnp.int32) * BQ + BQ - 1) // BK
    kb_lo = jnp.maximum(seg_start[firsts] // BK, kb_hi - (new_steps - 1))
    n_new = kb_hi - kb_lo + 1
    n_old = lasts - firsts + 1
    t = jnp.arange(steps, dtype=jnp.int32)[None, :]
    new_idx = (kb_lo[:, None] + jnp.minimum(t, n_new[:, None] - 1)).reshape(-1)
    old_idx = (firsts[:, None] + jnp.clip(t - n_new[:, None], 0, n_old[:, None] - 1)).reshape(-1)
    counts = jnp.stack([n_new, n_old], axis=1).reshape(-1)
    q2 = q_rows.reshape(n_q, BQ, 2, HD).transpose(0, 2, 1, 3).reshape(n_q, 2 * BQ, HD)
    seg_q = jnp.broadcast_to(seg_all.reshape(n_q, 1, BQ, 1), (n_q, 2, BQ, LANES)).reshape(n_q, 2 * BQ, LANES)
    seg_k = jnp.broadcast_to(seg_all.reshape(tokens // BK, 1, BK), (tokens // BK, 8, BK))
    cached = kv_cached.reshape(slots, cache_max, 2 * HD)

    def kernel(new_sm, old_sm, cnt_sm, len_sm, q_ref, segq_ref, kn_ref, vn_ref, segk_ref, kc_ref, vc_ref, o_ref,
               m_ref, l_ref, acc_ref):
        b = pl.program_id(0)
        step = pl.program_id(1)
        nn = cnt_sm[2 * b]
        no = cnt_sm[2 * b + 1]

        @pl.when(step == 0)
        def _():
            m_ref[...] = jnp.full(m_ref.shape, -1e30, jnp.float32)
            l_ref[...] = jnp.zeros(l_ref.shape, jnp.float32)
            acc_ref[...] = jnp.zeros(acc_ref.shape, jnp.float32)

        def widen(x, width):
            return x if width == LANES else jnp.concatenate([x] * (width // LANES), axis=1)

        def visit(s, v):
            m = m_ref[...]
            m_new = jnp.maximum(m, jnp.max(s, axis=1, keepdims=True))
            alpha = jnp.exp(m - m_new)
            p = jnp.exp(s - widen(m_new, s.shape[1]))
            l_ref[...] = l_ref[...] * alpha + jnp.sum(p, axis=1, keepdims=True)
            acc_ref[...] = acc_ref[...] * alpha + jnp.dot(
                p.astype(jnp.bfloat16), v, preferred_element_type=jnp.float32)
            m_ref[...] = m_new

        q = q_ref[0]
        sq = segq_ref[0]

        @pl.when(step < nn)
        def _():
            kb = new_sm[b * steps + step]
            s = lax.dot_general(q, kn_ref[...], (((1,), (1,)), ((), ())),
                                preferred_element_type=jnp.float32) * scale
            rows = lax.broadcasted_iota(jnp.int32, s.shape, 0)
            cols = lax.broadcasted_iota(jnp.int32, s.shape, 1)
            qpos = b * BQ + jnp.bitwise_and(rows, BQ - 1)
            vis = (sq == segk_ref[0][:1, :]) & (kb * BK + cols <= qpos)
            visit(jnp.where(vis, s, -jnp.inf), vn_ref[...])

        @pl.when((step >= nn) & (step < nn + no))
        def _():
            r = old_sm[b * steps + step]
            s = lax.dot_general(q, kc_ref[0], (((1,), (1,)), ((), ())),
                                preferred_element_type=jnp.float32) * scale
            cols = lax.broadcasted_iota(jnp.int32, s.shape, 1)
            vis = (widen(sq, s.shape[1]) == r) & (cols < len_sm[r])
            visit(jnp.where(vis, s, -jnp.inf), vc_ref[0])

        @pl.when(step == steps - 1)
        def _():
            o_ref[0] = (acc_ref[...] / l_ref[...]).astype(jnp.bfloat16)

    def at(table):
        return lambda b, t, new_sm, old_sm, cnt_sm, len_sm: table(b, t, new_sm, old_sm)

    grid_spec = pltpu.PrefetchScalarGridSpec(
        num_scalar_prefetch=4,
        grid=(n_q, steps),
        in_specs=[
            pl.BlockSpec((1, 2 * BQ, HD), lambda b, t2, *_: (b, 0, 0)),
            pl.BlockSpec((1, 2 * BQ, LANES), lambda b, t2, *_: (b, 0, 0)),
            pl.BlockSpec((BK, HD), at(lambda b, t, n, o: (n[b * steps + t], 0))),
            pl.BlockSpec((BK, HD), at(lambda b, t, n, o: (n[b * steps + t], 1))),
            pl.BlockSpec((1, 8, BK), at(lambda b, t, n, o: (n[b * steps + t], 0, 0))),
            pl.BlockSpec((1, cache_max, HD), at(lambda b, t, n, o: (o[b * steps + t], 0, 0))),
            pl.BlockSpec((1, cache_max, HD), at(lambda b, t, n, o: (o[b * steps + t], 0, 1))),
        ],
        out_specs=pl.BlockSpec((1, 2 * BQ, HD), lambda b, t2, *_: (b, 0, 0)),
        scratch_shapes=[
            pltpu.VMEM((2 * BQ, LANES), jnp.float32),
            pltpu.VMEM((2 * BQ, LANES), jnp.float32),
            pltpu.VMEM((2 * BQ, HD), jnp.float32),
        ],
    )
    out = pl.pallas_call(
        kernel,
        grid_spec=grid_spec,
        out_shape=jax.ShapeDtypeStruct((n_q, 2 * BQ, HD), jnp.bfloat16),
    )(new_idx, old_idx, counts, lengths, q2, seg_q, kv_new, kv_new, seg_k, cached, cached)
    return out.reshape(n_q, 2, BQ, HD).transpose(0, 2, 1, 3).reshape(tokens, 2 * HD)


def expert_apply(rows_in, expert_in, expert_out):
    dims_in = rows_in.shape
    flat = rows_in.reshape(-1, dims_in[-1])
    both = jnp.dot(flat, expert_in[0], preferred_element_type=jnp.float32)
    half_units = both.shape[1] // 2
    hidden = (jax.nn.silu(both[:, :half_units]) * both[:, half_units:]).astype(jnp.bfloat16)
    half_out = jnp.dot(hidden, expert_out[0], preferred_element_type=jnp.float32)
    return half_out.reshape(dims_in)


def shards(
    tokens,
    queries,
    new_kv,
    page_pool,
    seg_ids,
    cache_len,
    page_table,
    moves,
    out_weight,
    norm_gain,
    expert_ids,
    gate_weights,
    expert_in,
    expert_out,
):
    n_wide = lax.axis_size("wide")
    n_narrow = lax.axis_size("y") * lax.axis_size("core")
    my_group = lax.axis_index("wide")
    tok_dev, width = tokens.shape
    group_tok = tok_dev * n_narrow
    requests = moves.shape[0]
    page_rows = page_pool.shape[1]
    kv_feat = page_pool.shape[2]
    pages_each = page_pool.shape[0] // requests
    heads_here = QH // n_narrow
    group_size = QH // KVH
    ranks = rank_among_equal(moves)
    offsets = jnp.arange(n_wide, dtype=jnp.int32)
    places = jnp.arange(PAGE_CAP, dtype=jnp.int32)
    slot_hits = (moves[None, None, :] == offsets[:, None, None]) & (
        ranks[None, None, :] == places[None, :, None]
    )
    picked = jnp.sum(slot_hits.astype(jnp.int32) * jnp.arange(requests, dtype=jnp.int32), axis=2)
    filled = jnp.any(slot_hits, axis=2)
    by_dest = (offsets - my_group) % n_wide
    picked = picked[by_dest]
    filled = filled[by_dest]
    blocks = page_pool.reshape(requests, pages_each * page_rows, kv_feat)
    outgoing = jnp.take(blocks, picked.reshape(-1), axis=0).reshape(
        n_wide, PAGE_CAP, pages_each * page_rows, kv_feat
    )
    outgoing = jnp.where(filled[:, :, None, None], outgoing, jnp.zeros((), outgoing.dtype))
    arrived = lax.all_to_all(outgoing, "wide", split_axis=0, concat_axis=0, tiled=True)
    sources = (my_group - moves) % n_wide
    first_page = (sources * PAGE_CAP + ranks) * pages_each
    page_index = (first_page[:, None] + page_table[0]).reshape(-1)
    arrived = arrived.reshape(n_wide * PAGE_CAP * pages_each, page_rows, kv_feat)
    cached = jnp.take(arrived, page_index, axis=0)
    kv_of_dest = jnp.arange(n_narrow, dtype=jnp.int32) * heads_here // group_size
    q_send = queries.reshape(1, tok_dev, n_narrow, heads_here * HD)
    kv_send = jnp.take(new_kv.reshape(tok_dev, KVH, 2 * HD), kv_of_dest, axis=1).reshape(
        1, tok_dev, n_narrow, 2 * HD
    )
    cache_send = jnp.take(
        cached.reshape(requests * pages_each, page_rows, KVH, 2 * HD), kv_of_dest, axis=2
    )
    q_heads, kv_heads, cache_heads = (
        lax.all_to_all(q_send, NARROW, split_axis=2, concat_axis=1, tiled=True),
        lax.all_to_all(kv_send, NARROW, split_axis=2, concat_axis=1, tiled=True),
        lax.all_to_all(cache_send, NARROW, split_axis=2, concat_axis=1, tiled=True),
    )
    q_heads = q_heads.reshape(group_tok, heads_here, HD)
    kv_heads = kv_heads.reshape(group_tok, 2 * HD)
    cache_max = pages_each * page_rows * n_narrow
    cache_heads = cache_heads.reshape(requests * cache_max, 2 * HD)
    key_new = kv_heads[:, :HD]
    value_new = kv_heads[:, HD:]
    key_cached = cache_heads[:, :HD]
    value_cached = cache_heads[:, HD:]
    seg_all = seg_ids[0]
    lengths = cache_len[0]
    attended = slot_attention(
        q_heads.reshape(group_tok, heads_here * HD), kv_heads, cache_heads, seg_all, lengths, cache_max
    ).reshape(n_narrow, tok_dev, heads_here * HD)
    back_home = lax.all_to_all(attended, NARROW, split_axis=0, concat_axis=2, tiled=True)
    mixed = back_home.reshape(tok_dev, QH * HD)
    residual = tokens.astype(jnp.float32) + jnp.dot(
        mixed, out_weight, preferred_element_type=jnp.float32
    )
    scale_row = lax.rsqrt(jnp.mean(residual * residual, axis=-1, keepdims=True) + norm_eps)
    normed = (residual * scale_row * norm_gain).astype(jnp.bfloat16)
    experts = n_wide * n_narrow // 2
    capacity = tok_dev * TOPK * 4 // (3 * experts)
    flat_ids = expert_ids.reshape(-1)
    onehot = (flat_ids[:, None] == jnp.arange(experts, dtype=jnp.int32)[None, :]).astype(jnp.int32)
    before = jnp.cumsum(onehot, axis=0) - onehot
    slot_place = jnp.sum(before * onehot, axis=1)
    slot_of = flat_ids * capacity + slot_place
    token_of = jnp.arange(tok_dev * TOPK, dtype=jnp.int32) // TOPK
    slot_token = jnp.zeros((experts * capacity,), jnp.int32).at[slot_of].set(token_of)
    slot_used = jnp.zeros((experts * capacity,), jnp.bool_).at[slot_of].set(True)
    outgoing_rows = jnp.where(
        slot_used[:, None], jnp.take(normed, slot_token, axis=0), jnp.zeros((), jnp.bfloat16)
    )
    outgoing_rows = outgoing_rows.reshape(experts, capacity, width)
    at_chip = lax.all_to_all(outgoing_rows, CHIPS, split_axis=0, concat_axis=0, tiled=True)
    both_cores = lax.all_gather(at_chip, "core", axis=0, tiled=False)
    half_out = expert_apply(both_cores, expert_in, expert_out)
    core = lax.axis_index("core")
    mine = lax.dynamic_index_in_dim(half_out, core, 0, keepdims=False)
    theirs = lax.dynamic_index_in_dim(half_out, 1 - core, 0, keepdims=False)
    partner = lax.ppermute(theirs, "core", perm=[(0, 1), (1, 0)])
    summed = (mine + partner).astype(jnp.bfloat16)
    returned = lax.all_to_all(summed, CHIPS, split_axis=0, concat_axis=0, tiled=True)
    summed_rows = returned.reshape(experts * capacity, width)
    picked_rows = jnp.take(summed_rows, slot_of, axis=0)
    weighted = picked_rows.astype(jnp.float32) * gate_weights.reshape(-1)[:, None]
    expert_sum = jnp.sum(weighted.reshape(tok_dev, TOPK, width), axis=1)
    return (residual + expert_sum).astype(jnp.bfloat16)


def solution(mesh):
    placed = (
        P(WN, None),
        P(WN, None),
        P(WN, None),
        P("wide", NARROW, None),
        P("wide", None),
        P("wide", None),
        P("wide", None, None),
        P(),
        P(),
        P(),
        P(WN, None),
        P(WN, None),
        P(WN, None, None),
        P(WN, None, None),
    )
    mesh = Mesh(mesh.devices.reshape(mesh.shape["wide"], -1, 2), ("wide", "y", "core"))
    return jax.shard_map(
        shards, mesh=mesh, in_specs=placed, out_specs=P(WN, None), check_vma=False
    )
```

```python
import functools

import jax
import jax.numpy as jnp
from jax import lax
from jax.experimental import pallas as pl
from jax.experimental.pallas import tpu as pltpu
from jax.sharding import Mesh
from jax.sharding import PartitionSpec as P

QH = 16
KVH = 4
HD = 128
TOPK = 6
PAGE_CAP = 2
NARROW = ("y", "core")
CHIPS = ("wide", "y")
WN = ("wide", "y", "core")


norm_eps = 1e-06
block_limit = 512
BQ = 128
BK = 128
LANES = 128


def rank_among_equal(values):
    length = values.shape[0]
    order = jnp.arange(length, dtype=jnp.int32)
    earlier = (values[None, :] == values[:, None]) & (order[None, :] < order[:, None])
    return jnp.sum(earlier.astype(jnp.int32), axis=1)


def block_scores(q_block, keys):
    return jnp.einsum("bhd,kd->hbk", q_block, keys, preferred_element_type=jnp.float32) * HD ** (
        -0.5
    )


def fresh_scores(start_row, q_heads, key_new, seg_all, block_len):
    q_block = lax.dynamic_slice_in_dim(q_heads, start_row, block_len, 0)
    seg_block = lax.dynamic_slice_in_dim(seg_all, start_row, block_len, 0)
    row_pos = start_row + jnp.arange(block_len, dtype=jnp.int32)
    positions = jnp.arange(seg_all.shape[0], dtype=jnp.int32)
    visible = (seg_block[:, None] == seg_all[None, :]) & (positions[None, :] <= row_pos[:, None])
    scores = jnp.where(visible[None], block_scores(q_block, key_new), -jnp.inf)
    return (q_block, seg_block, scores)


def attend_masked(
    start_row,
    q_heads,
    key_new,
    value_new,
    key_cached,
    value_cached,
    seg_all,
    lengths,
    cache_max,
    block_len,
):
    q_block, seg_block, fresh = fresh_scores(start_row, q_heads, key_new, seg_all, block_len)
    key_req = jnp.arange(key_cached.shape[0], dtype=jnp.int32) // cache_max
    key_pos = jnp.arange(key_cached.shape[0], dtype=jnp.int32) % cache_max
    visible = (seg_block[:, None] == key_req[None, :]) & (
        key_pos[None, :] < lengths[key_req][None, :]
    )
    older = jnp.where(visible[None], block_scores(q_block, key_cached), -jnp.inf)
    row_max = jnp.maximum(jnp.max(fresh, axis=-1), jnp.max(older, axis=-1))
    fresh_exp = jnp.exp(fresh - row_max[..., None])
    older_exp = jnp.exp(older - row_max[..., None])
    row_total = jnp.sum(fresh_exp, axis=-1) + jnp.sum(older_exp, axis=-1)
    fresh_w = (fresh_exp / row_total[..., None]).astype(jnp.bfloat16)
    older_w = (older_exp / row_total[..., None]).astype(jnp.bfloat16)
    attended = jnp.einsum("hbk,kd->bhd", fresh_w, value_new, preferred_element_type=jnp.float32)
    attended = attended + jnp.einsum(
        "hbk,kd->bhd", older_w, value_cached, preferred_element_type=jnp.float32
    )
    return attended.astype(jnp.bfloat16).reshape(block_len, -1)


def slot_attention(q_rows, kv_new, kv_cached, seg_all, lengths, cache_max):
    tokens = q_rows.shape[0]
    slots = lengths.shape[0]
    scale = HD ** (-0.5)
    n_q = tokens // BQ
    new_steps = (cache_max + BQ) // BK
    steps = new_steps + slots
    seg_start = jnp.sum(
        (seg_all[None, :] < jnp.arange(slots, dtype=jnp.int32)[:, None]).astype(jnp.int32), axis=1
    )
    firsts = seg_all[::BQ]
    lasts = seg_all[BQ - 1 :: BQ]
    kb_hi = (jnp.arange(n_q, dtype=jnp.int32) * BQ + BQ - 1) // BK
    kb_lo = jnp.maximum(seg_start[firsts] // BK, kb_hi - (new_steps - 1))
    n_new = kb_hi - kb_lo + 1
    n_old = lasts - firsts + 1
    t = jnp.arange(steps, dtype=jnp.int32)[None, :]
    new_idx = (kb_lo[:, None] + jnp.minimum(t, n_new[:, None] - 1)).reshape(-1)
    old_idx = (firsts[:, None] + jnp.clip(t - n_new[:, None], 0, n_old[:, None] - 1)).reshape(-1)
    counts = jnp.stack([n_new, n_old], axis=1).reshape(-1)
    q2 = q_rows.reshape(n_q, BQ, 2, HD).transpose(0, 2, 1, 3).reshape(n_q, 2 * BQ, HD)
    seg_q = jnp.broadcast_to(seg_all.reshape(n_q, 1, BQ, 1), (n_q, 2, BQ, LANES)).reshape(n_q, 2 * BQ, LANES)
    seg_k = jnp.broadcast_to(seg_all.reshape(tokens // BK, 1, BK), (tokens // BK, 8, BK))
    cached = kv_cached.reshape(slots, cache_max, 2 * HD)

    def kernel(new_sm, old_sm, cnt_sm, len_sm, q_ref, segq_ref, kn_ref, vn_ref, segk_ref, kc_ref, vc_ref, o_ref,
               m_ref, l_ref, acc_ref):
        b = pl.program_id(0)
        step = pl.program_id(1)
        nn = cnt_sm[2 * b]
        no = cnt_sm[2 * b + 1]

        @pl.when(step == 0)
        def _():
            m_ref[...] = jnp.full(m_ref.shape, -1e30, jnp.float32)
            l_ref[...] = jnp.zeros(l_ref.shape, jnp.float32)
            acc_ref[...] = jnp.zeros(acc_ref.shape, jnp.float32)

        def widen(x, width):
            return x if width == LANES else jnp.concatenate([x] * (width // LANES), axis=1)

        def visit(s, v):
            m = m_ref[...]
            m_new = jnp.maximum(m, jnp.max(s, axis=1, keepdims=True))
            alpha = jnp.exp(m - m_new)
            p = jnp.exp(s - widen(m_new, s.shape[1]))
            l_ref[...] = l_ref[...] * alpha + jnp.sum(p, axis=1, keepdims=True)
            acc_ref[...] = acc_ref[...] * alpha + jnp.dot(
                p.astype(jnp.bfloat16), v, preferred_element_type=jnp.float32)
            m_ref[...] = m_new

        q = q_ref[0]
        sq = segq_ref[0]

        @pl.when(step < nn)
        def _():
            kb = new_sm[b * steps + step]
            s = lax.dot_general(q, kn_ref[...], (((1,), (1,)), ((), ())),
                                preferred_element_type=jnp.float32) * scale
            rows = lax.broadcasted_iota(jnp.int32, s.shape, 0)
            cols = lax.broadcasted_iota(jnp.int32, s.shape, 1)
            qpos = b * BQ + jnp.bitwise_and(rows, BQ - 1)
            vis = (sq == segk_ref[0][:1, :]) & (kb * BK + cols <= qpos)
            visit(jnp.where(vis, s, -jnp.inf), vn_ref[...])

        @pl.when((step >= nn) & (step < nn + no))
        def _():
            r = old_sm[b * steps + step]
            s = lax.dot_general(q, kc_ref[0], (((1,), (1,)), ((), ())),
                                preferred_element_type=jnp.float32) * scale
            cols = lax.broadcasted_iota(jnp.int32, s.shape, 1)
            vis = (widen(sq, s.shape[1]) == r) & (cols < len_sm[r])
            visit(jnp.where(vis, s, -jnp.inf), vc_ref[0])

        @pl.when(step == steps - 1)
        def _():
            o_ref[0] = (acc_ref[...] / l_ref[...]).astype(jnp.bfloat16)

    def at(table):
        return lambda b, t, new_sm, old_sm, cnt_sm, len_sm: table(b, t, new_sm, old_sm)

    grid_spec = pltpu.PrefetchScalarGridSpec(
        num_scalar_prefetch=4,
        grid=(n_q, steps),
        in_specs=[
            pl.BlockSpec((1, 2 * BQ, HD), lambda b, t2, *_: (b, 0, 0)),
            pl.BlockSpec((1, 2 * BQ, LANES), lambda b, t2, *_: (b, 0, 0)),
            pl.BlockSpec((BK, HD), at(lambda b, t, n, o: (n[b * steps + t], 0))),
            pl.BlockSpec((BK, HD), at(lambda b, t, n, o: (n[b * steps + t], 1))),
            pl.BlockSpec((1, 8, BK), at(lambda b, t, n, o: (n[b * steps + t], 0, 0))),
            pl.BlockSpec((1, cache_max, HD), at(lambda b, t, n, o: (o[b * steps + t], 0, 0))),
            pl.BlockSpec((1, cache_max, HD), at(lambda b, t, n, o: (o[b * steps + t], 0, 1))),
        ],
        out_specs=pl.BlockSpec((1, 2 * BQ, HD), lambda b, t2, *_: (b, 0, 0)),
        scratch_shapes=[
            pltpu.VMEM((2 * BQ, LANES), jnp.float32),
            pltpu.VMEM((2 * BQ, LANES), jnp.float32),
            pltpu.VMEM((2 * BQ, HD), jnp.float32),
        ],
    )
    out = pl.pallas_call(
        kernel,
        grid_spec=grid_spec,
        out_shape=jax.ShapeDtypeStruct((n_q, 2 * BQ, HD), jnp.bfloat16),
    )(new_idx, old_idx, counts, lengths, q2, seg_q, kv_new, kv_new, seg_k, cached, cached)
    return out.reshape(n_q, 2, BQ, HD).transpose(0, 2, 1, 3).reshape(tokens, 2 * HD)


def expert_apply(rows_in, expert_in, expert_out):
    dims_in = rows_in.shape
    flat = rows_in.reshape(-1, dims_in[-1])
    both = jnp.dot(flat, expert_in[0], preferred_element_type=jnp.float32)
    half_units = both.shape[1] // 2
    hidden = (jax.nn.silu(both[:, :half_units]) * both[:, half_units:]).astype(jnp.bfloat16)
    half_out = jnp.dot(hidden, expert_out[0], preferred_element_type=jnp.float32)
    return half_out.reshape(dims_in)


def shards(
    tokens,
    queries,
    new_kv,
    page_pool,
    seg_ids,
    cache_len,
    page_table,
    moves,
    out_weight,
    norm_gain,
    expert_ids,
    gate_weights,
    expert_in,
    expert_out,
):
    n_wide = lax.axis_size("wide")
    n_narrow = lax.axis_size("y") * lax.axis_size("core")
    my_group = lax.axis_index("wide")
    tok_dev, width = tokens.shape
    group_tok = tok_dev * n_narrow
    requests = moves.shape[0]
    page_rows = page_pool.shape[1]
    kv_feat = page_pool.shape[2]
    pages_each = page_pool.shape[0] // requests
    heads_here = QH // n_narrow
    group_size = QH // KVH
    ranks = rank_among_equal(moves)
    offsets = jnp.arange(n_wide, dtype=jnp.int32)
    places = jnp.arange(PAGE_CAP, dtype=jnp.int32)
    slot_hits = (moves[None, None, :] == offsets[:, None, None]) & (
        ranks[None, None, :] == places[None, :, None]
    )
    picked = jnp.sum(slot_hits.astype(jnp.int32) * jnp.arange(requests, dtype=jnp.int32), axis=2)
    filled = jnp.any(slot_hits, axis=2)
    by_dest = (offsets - my_group) % n_wide
    picked = picked[by_dest]
    filled = filled[by_dest]
    blocks = page_pool.reshape(requests, pages_each * page_rows, kv_feat)
    outgoing = jnp.take(blocks, picked.reshape(-1), axis=0).reshape(
        n_wide, PAGE_CAP, pages_each * page_rows, kv_feat
    )
    outgoing = jnp.where(filled[:, :, None, None], outgoing, jnp.zeros((), outgoing.dtype))
    arrived = lax.all_to_all(outgoing, "wide", split_axis=0, concat_axis=0, tiled=True)
    sources = (my_group - moves) % n_wide
    first_page = (sources * PAGE_CAP + ranks) * pages_each
    page_index = (first_page[:, None] + page_table[0]).reshape(-1)
    arrived = arrived.reshape(n_wide * PAGE_CAP * pages_each, page_rows, kv_feat)
    cached = jnp.take(arrived, page_index, axis=0)
    kv_of_dest = jnp.arange(n_narrow, dtype=jnp.int32) * heads_here // group_size
    q_send = queries.reshape(1, tok_dev, n_narrow, heads_here * HD)
    kv_send = jnp.take(new_kv.reshape(tok_dev, KVH, 2 * HD), kv_of_dest, axis=1).reshape(
        1, tok_dev, n_narrow, 2 * HD
    )
    cache_send = jnp.take(
        cached.reshape(requests * pages_each, page_rows, KVH, 2 * HD), kv_of_dest, axis=2
    )
    q_heads, kv_heads, cache_heads = (
        lax.all_to_all(q_send, NARROW, split_axis=2, concat_axis=1, tiled=True),
        lax.all_to_all(kv_send, NARROW, split_axis=2, concat_axis=1, tiled=True),
        lax.all_to_all(cache_send, NARROW, split_axis=2, concat_axis=1, tiled=True),
    )
    q_heads = q_heads.reshape(group_tok, heads_here, HD)
    kv_heads = kv_heads.reshape(group_tok, 2 * HD)
    cache_max = pages_each * page_rows * n_narrow
    cache_heads = cache_heads.reshape(requests * cache_max, 2 * HD)
    key_new = kv_heads[:, :HD]
    value_new = kv_heads[:, HD:]
    key_cached = cache_heads[:, :HD]
    value_cached = cache_heads[:, HD:]
    seg_all = seg_ids[0]
    lengths = cache_len[0]
    attended = slot_attention(
        q_heads.reshape(group_tok, heads_here * HD), kv_heads, cache_heads, seg_all, lengths, cache_max
    ).reshape(n_narrow, tok_dev, heads_here * HD)
    back_home = lax.all_to_all(attended, NARROW, split_axis=0, concat_axis=2, tiled=True)
    mixed = back_home.reshape(tok_dev, QH * HD)
    residual = tokens.astype(jnp.float32) + jnp.dot(
        mixed, out_weight, preferred_element_type=jnp.float32
    )
    scale_row = lax.rsqrt(jnp.mean(residual * residual, axis=-1, keepdims=True) + norm_eps)
    normed = (residual * scale_row * norm_gain).astype(jnp.bfloat16)
    experts = n_wide * n_narrow // 2
    capacity = tok_dev * TOPK * 4 // (3 * experts)
    flat_ids = expert_ids.reshape(-1)
    onehot = (flat_ids[:, None] == jnp.arange(experts, dtype=jnp.int32)[None, :]).astype(jnp.int32)
    before = jnp.cumsum(onehot, axis=0) - onehot
    slot_place = jnp.sum(before * onehot, axis=1)
    slot_of = flat_ids * capacity + slot_place
    token_of = jnp.arange(tok_dev * TOPK, dtype=jnp.int32) // TOPK
    slot_token = jnp.zeros((experts * capacity,), jnp.int32).at[slot_of].set(token_of)
    slot_used = jnp.zeros((experts * capacity,), jnp.bool_).at[slot_of].set(True)
    outgoing_rows = jnp.where(
        slot_used[:, None], jnp.take(normed, slot_token, axis=0), jnp.zeros((), jnp.bfloat16)
    )
    outgoing_rows = outgoing_rows.reshape(experts, capacity, width)
    at_chip = lax.all_to_all(outgoing_rows, CHIPS, split_axis=0, concat_axis=0, tiled=True)
    swap = [(0, 1), (1, 0)]
    partner_rows = lax.ppermute(at_chip, "core", perm=swap)
    own_half = expert_apply(at_chip, expert_in, expert_out)
    own_half, partner_rows = lax.optimization_barrier((own_half, partner_rows))
    partner_half = expert_apply(partner_rows, expert_in, expert_out)
    other_half = lax.ppermute(partner_half, "core", perm=swap)
    summed = (own_half + other_half).astype(jnp.bfloat16)
    returned = lax.all_to_all(summed, CHIPS, split_axis=0, concat_axis=0, tiled=True)
    summed_rows = returned.reshape(experts * capacity, width)
    picked_rows = jnp.take(summed_rows, slot_of, axis=0)
    weighted = picked_rows.astype(jnp.float32) * gate_weights.reshape(-1)[:, None]
    expert_sum = jnp.sum(weighted.reshape(tok_dev, TOPK, width), axis=1)
    return (residual + expert_sum).astype(jnp.bfloat16)


def solution(mesh):
    placed = (
        P(WN, None),
        P(WN, None),
        P(WN, None),
        P("wide", NARROW, None),
        P("wide", None),
        P("wide", None),
        P("wide", None, None),
        P(),
        P(),
        P(),
        P(WN, None),
        P(WN, None),
        P(WN, None, None),
        P(WN, None, None),
    )
    mesh = Mesh(mesh.devices.reshape(mesh.shape["wide"], -1, 2), ("wide", "y", "core"))
    return jax.shard_map(
        shards, mesh=mesh, in_specs=placed, out_specs=P(WN, None), check_vma=False
    )
```

```python
import functools

import jax
import jax.numpy as jnp
from jax import lax
from jax.experimental import pallas as pl
from jax.experimental.pallas import tpu as pltpu
from jax.sharding import Mesh
from jax.sharding import PartitionSpec as P

QH = 16
KVH = 4
HD = 128
TOPK = 6
PAGE_CAP = 2
NARROW = ("y", "core")
CHIPS = ("wide", "y")
WN = ("wide", "y", "core")


norm_eps = 1e-06
block_limit = 512
BQ = 128
BK = 128
LANES = 128


def rank_among_equal(values):
    length = values.shape[0]
    order = jnp.arange(length, dtype=jnp.int32)
    earlier = (values[None, :] == values[:, None]) & (order[None, :] < order[:, None])
    return jnp.sum(earlier.astype(jnp.int32), axis=1)


def block_scores(q_block, keys):
    return jnp.einsum("bhd,kd->hbk", q_block, keys, preferred_element_type=jnp.float32) * HD ** (
        -0.5
    )


def fresh_scores(start_row, q_heads, key_new, seg_all, block_len):
    q_block = lax.dynamic_slice_in_dim(q_heads, start_row, block_len, 0)
    seg_block = lax.dynamic_slice_in_dim(seg_all, start_row, block_len, 0)
    row_pos = start_row + jnp.arange(block_len, dtype=jnp.int32)
    positions = jnp.arange(seg_all.shape[0], dtype=jnp.int32)
    visible = (seg_block[:, None] == seg_all[None, :]) & (positions[None, :] <= row_pos[:, None])
    scores = jnp.where(visible[None], block_scores(q_block, key_new), -jnp.inf)
    return (q_block, seg_block, scores)


def attend_masked(
    start_row,
    q_heads,
    key_new,
    value_new,
    key_cached,
    value_cached,
    seg_all,
    lengths,
    cache_max,
    block_len,
):
    q_block, seg_block, fresh = fresh_scores(start_row, q_heads, key_new, seg_all, block_len)
    key_req = jnp.arange(key_cached.shape[0], dtype=jnp.int32) // cache_max
    key_pos = jnp.arange(key_cached.shape[0], dtype=jnp.int32) % cache_max
    visible = (seg_block[:, None] == key_req[None, :]) & (
        key_pos[None, :] < lengths[key_req][None, :]
    )
    older = jnp.where(visible[None], block_scores(q_block, key_cached), -jnp.inf)
    row_max = jnp.maximum(jnp.max(fresh, axis=-1), jnp.max(older, axis=-1))
    fresh_exp = jnp.exp(fresh - row_max[..., None])
    older_exp = jnp.exp(older - row_max[..., None])
    row_total = jnp.sum(fresh_exp, axis=-1) + jnp.sum(older_exp, axis=-1)
    fresh_w = (fresh_exp / row_total[..., None]).astype(jnp.bfloat16)
    older_w = (older_exp / row_total[..., None]).astype(jnp.bfloat16)
    attended = jnp.einsum("hbk,kd->bhd", fresh_w, value_new, preferred_element_type=jnp.float32)
    attended = attended + jnp.einsum(
        "hbk,kd->bhd", older_w, value_cached, preferred_element_type=jnp.float32
    )
    return attended.astype(jnp.bfloat16).reshape(block_len, -1)


def slot_attention(q_rows, kv_new, kv_cached, seg_all, lengths, cache_max):
    tokens = q_rows.shape[0]
    slots = lengths.shape[0]
    scale = HD ** (-0.5)
    n_q = tokens // BQ
    new_steps = (cache_max + BQ) // BK
    steps = new_steps + slots
    seg_start = jnp.sum(
        (seg_all[None, :] < jnp.arange(slots, dtype=jnp.int32)[:, None]).astype(jnp.int32), axis=1
    )
    firsts = seg_all[::BQ]
    lasts = seg_all[BQ - 1 :: BQ]
    kb_hi = (jnp.arange(n_q, dtype=jnp.int32) * BQ + BQ - 1) // BK
    kb_lo = jnp.maximum(seg_start[firsts] // BK, kb_hi - (new_steps - 1))
    n_new = kb_hi - kb_lo + 1
    n_old = lasts - firsts + 1
    t = jnp.arange(steps, dtype=jnp.int32)[None, :]
    new_idx = (kb_lo[:, None] + jnp.minimum(t, n_new[:, None] - 1)).reshape(-1)
    old_idx = (firsts[:, None] + jnp.clip(t - n_new[:, None], 0, n_old[:, None] - 1)).reshape(-1)
    counts = jnp.stack([n_new, n_old], axis=1).reshape(-1)
    q2 = q_rows.reshape(n_q, BQ, 2, HD).transpose(0, 2, 1, 3).reshape(n_q, 2 * BQ, HD)
    seg_q = jnp.broadcast_to(seg_all.reshape(n_q, 1, BQ, 1), (n_q, 2, BQ, LANES)).reshape(n_q, 2 * BQ, LANES)
    seg_k = jnp.broadcast_to(seg_all.reshape(tokens // BK, 1, BK), (tokens // BK, 8, BK))
    cached = kv_cached.reshape(slots, cache_max, 2 * HD)

    def kernel(new_sm, old_sm, cnt_sm, len_sm, q_ref, segq_ref, kn_ref, vn_ref, segk_ref, kc_ref, vc_ref, o_ref,
               m_ref, l_ref, acc_ref):
        b = pl.program_id(0)
        step = pl.program_id(1)
        nn = cnt_sm[2 * b]
        no = cnt_sm[2 * b + 1]

        @pl.when(step == 0)
        def _():
            m_ref[...] = jnp.full(m_ref.shape, -1e30, jnp.float32)
            l_ref[...] = jnp.zeros(l_ref.shape, jnp.float32)
            acc_ref[...] = jnp.zeros(acc_ref.shape, jnp.float32)

        def widen(x, width):
            return x if width == LANES else jnp.concatenate([x] * (width // LANES), axis=1)

        def visit(s, v):
            m = m_ref[...]
            m_new = jnp.maximum(m, jnp.max(s, axis=1, keepdims=True))
            alpha = jnp.exp(m - m_new)
            p = jnp.exp(s - widen(m_new, s.shape[1]))
            l_ref[...] = l_ref[...] * alpha + jnp.sum(p, axis=1, keepdims=True)
            acc_ref[...] = acc_ref[...] * alpha + jnp.dot(
                p.astype(jnp.bfloat16), v, preferred_element_type=jnp.float32)
            m_ref[...] = m_new

        q = q_ref[0]
        sq = segq_ref[0]

        @pl.when(step < nn)
        def _():
            kb = new_sm[b * steps + step]
            s = lax.dot_general(q, kn_ref[...], (((1,), (1,)), ((), ())),
                                preferred_element_type=jnp.float32) * scale
            rows = lax.broadcasted_iota(jnp.int32, s.shape, 0)
            cols = lax.broadcasted_iota(jnp.int32, s.shape, 1)
            qpos = b * BQ + jnp.bitwise_and(rows, BQ - 1)
            vis = (sq == segk_ref[0][:1, :]) & (kb * BK + cols <= qpos)
            visit(jnp.where(vis, s, -jnp.inf), vn_ref[...])

        @pl.when((step >= nn) & (step < nn + no))
        def _():
            r = old_sm[b * steps + step]
            s = lax.dot_general(q, kc_ref[0], (((1,), (1,)), ((), ())),
                                preferred_element_type=jnp.float32) * scale
            cols = lax.broadcasted_iota(jnp.int32, s.shape, 1)
            vis = (widen(sq, s.shape[1]) == r) & (cols < len_sm[r])
            visit(jnp.where(vis, s, -jnp.inf), vc_ref[0])

        @pl.when(step == steps - 1)
        def _():
            o_ref[0] = (acc_ref[...] / l_ref[...]).astype(jnp.bfloat16)

    def at(table):
        return lambda b, t, new_sm, old_sm, cnt_sm, len_sm: table(b, t, new_sm, old_sm)

    grid_spec = pltpu.PrefetchScalarGridSpec(
        num_scalar_prefetch=4,
        grid=(n_q, steps),
        in_specs=[
            pl.BlockSpec((1, 2 * BQ, HD), lambda b, t2, *_: (b, 0, 0)),
            pl.BlockSpec((1, 2 * BQ, LANES), lambda b, t2, *_: (b, 0, 0)),
            pl.BlockSpec((BK, HD), at(lambda b, t, n, o: (n[b * steps + t], 0))),
            pl.BlockSpec((BK, HD), at(lambda b, t, n, o: (n[b * steps + t], 1))),
            pl.BlockSpec((1, 8, BK), at(lambda b, t, n, o: (n[b * steps + t], 0, 0))),
            pl.BlockSpec((1, cache_max, HD), at(lambda b, t, n, o: (o[b * steps + t], 0, 0))),
            pl.BlockSpec((1, cache_max, HD), at(lambda b, t, n, o: (o[b * steps + t], 0, 1))),
        ],
        out_specs=pl.BlockSpec((1, 2 * BQ, HD), lambda b, t2, *_: (b, 0, 0)),
        scratch_shapes=[
            pltpu.VMEM((2 * BQ, LANES), jnp.float32),
            pltpu.VMEM((2 * BQ, LANES), jnp.float32),
            pltpu.VMEM((2 * BQ, HD), jnp.float32),
        ],
    )
    out = pl.pallas_call(
        kernel,
        grid_spec=grid_spec,
        out_shape=jax.ShapeDtypeStruct((n_q, 2 * BQ, HD), jnp.bfloat16),
    )(new_idx, old_idx, counts, lengths, q2, seg_q, kv_new, kv_new, seg_k, cached, cached)
    return out.reshape(n_q, 2, BQ, HD).transpose(0, 2, 1, 3).reshape(tokens, 2 * HD)


def expert_apply(rows_in, expert_in, expert_out):
    dims_in = rows_in.shape
    flat = rows_in.reshape(-1, dims_in[-1])
    both = jnp.dot(flat, expert_in[0], preferred_element_type=jnp.float32)
    half_units = both.shape[1] // 2
    hidden = (jax.nn.silu(both[:, :half_units]) * both[:, half_units:]).astype(jnp.bfloat16)
    half_out = jnp.dot(hidden, expert_out[0], preferred_element_type=jnp.float32)
    return half_out.reshape(dims_in)


def shards(
    tokens,
    queries,
    new_kv,
    page_pool,
    seg_ids,
    cache_len,
    page_table,
    moves,
    out_weight,
    norm_gain,
    expert_ids,
    gate_weights,
    expert_in,
    expert_out,
):
    n_wide = lax.axis_size("wide")
    n_narrow = lax.axis_size("y") * lax.axis_size("core")
    my_group = lax.axis_index("wide")
    tok_dev, width = tokens.shape
    group_tok = tok_dev * n_narrow
    requests = moves.shape[0]
    page_rows = page_pool.shape[1]
    kv_feat = page_pool.shape[2]
    pages_each = page_pool.shape[0] // requests
    heads_here = QH // n_narrow
    group_size = QH // KVH
    ranks = rank_among_equal(moves)
    offsets = jnp.arange(n_wide, dtype=jnp.int32)
    places = jnp.arange(PAGE_CAP, dtype=jnp.int32)
    slot_hits = (moves[None, None, :] == offsets[:, None, None]) & (
        ranks[None, None, :] == places[None, :, None]
    )
    picked = jnp.sum(slot_hits.astype(jnp.int32) * jnp.arange(requests, dtype=jnp.int32), axis=2)
    filled = jnp.any(slot_hits, axis=2)
    by_dest = (offsets - my_group) % n_wide
    picked = picked[by_dest]
    filled = filled[by_dest]
    blocks = page_pool.reshape(requests, pages_each * page_rows, kv_feat)
    outgoing = jnp.take(blocks, picked.reshape(-1), axis=0).reshape(
        n_wide, PAGE_CAP, pages_each * page_rows, kv_feat
    )
    outgoing = jnp.where(filled[:, :, None, None], outgoing, jnp.zeros((), outgoing.dtype))
    arrived = lax.all_to_all(outgoing, "wide", split_axis=0, concat_axis=0, tiled=True)
    sources = (my_group - moves) % n_wide
    first_page = (sources * PAGE_CAP + ranks) * pages_each
    page_index = (first_page[:, None] + page_table[0]).reshape(-1)
    arrived = arrived.reshape(n_wide * PAGE_CAP * pages_each, page_rows, kv_feat)
    cached = jnp.take(arrived, page_index, axis=0)
    kv_of_dest = jnp.arange(n_narrow, dtype=jnp.int32) * heads_here // group_size
    q_send = queries.reshape(1, tok_dev, n_narrow, heads_here * HD)
    kv_send = jnp.take(new_kv.reshape(tok_dev, KVH, 2 * HD), kv_of_dest, axis=1).reshape(
        1, tok_dev, n_narrow, 2 * HD
    )
    cache_send = jnp.take(
        cached.reshape(requests * pages_each, page_rows, KVH, 2 * HD), kv_of_dest, axis=2
    )
    q_heads, kv_heads, cache_heads = (
        lax.all_to_all(q_send, NARROW, split_axis=2, concat_axis=1, tiled=True),
        lax.all_to_all(kv_send, NARROW, split_axis=2, concat_axis=1, tiled=True),
        lax.all_to_all(cache_send, NARROW, split_axis=2, concat_axis=1, tiled=True),
    )
    q_heads = q_heads.reshape(group_tok, heads_here, HD)
    kv_heads = kv_heads.reshape(group_tok, 2 * HD)
    cache_max = pages_each * page_rows * n_narrow
    cache_heads = cache_heads.reshape(requests * cache_max, 2 * HD)
    key_new = kv_heads[:, :HD]
    value_new = kv_heads[:, HD:]
    key_cached = cache_heads[:, :HD]
    value_cached = cache_heads[:, HD:]
    seg_all = seg_ids[0]
    lengths = cache_len[0]
    attended = slot_attention(
        q_heads.reshape(group_tok, heads_here * HD), kv_heads, cache_heads, seg_all, lengths, cache_max
    ).reshape(n_narrow, tok_dev, heads_here * HD)
    back_home = lax.all_to_all(attended, NARROW, split_axis=0, concat_axis=2, tiled=True)
    mixed = back_home.reshape(tok_dev, QH * HD)
    residual = tokens.astype(jnp.float32) + jnp.dot(
        mixed, out_weight, preferred_element_type=jnp.float32
    )
    scale_row = lax.rsqrt(jnp.mean(residual * residual, axis=-1, keepdims=True) + norm_eps)
    normed = (residual * scale_row * norm_gain).astype(jnp.bfloat16)
    experts = n_wide * n_narrow // 2
    capacity = tok_dev * TOPK * 4 // (3 * experts)
    flat_ids = expert_ids.reshape(-1)
    onehot = (flat_ids[:, None] == jnp.arange(experts, dtype=jnp.int32)[None, :]).astype(jnp.int32)
    before = jnp.cumsum(onehot, axis=0) - onehot
    slot_place = jnp.sum(before * onehot, axis=1)
    slot_of = flat_ids * capacity + slot_place
    token_of = jnp.arange(tok_dev * TOPK, dtype=jnp.int32) // TOPK
    slot_token = jnp.zeros((experts * capacity,), jnp.int32).at[slot_of].set(token_of)
    slot_used = jnp.zeros((experts * capacity,), jnp.bool_).at[slot_of].set(True)
    outgoing_rows = jnp.where(
        slot_used[:, None], jnp.take(normed, slot_token, axis=0), jnp.zeros((), jnp.bfloat16)
    )
    outgoing_rows = outgoing_rows.reshape(experts, capacity, width)
    at_chip = lax.all_to_all(outgoing_rows, CHIPS, split_axis=0, concat_axis=0, tiled=True)
    swap = [(0, 1), (1, 0)]
    partner_rows = lax.ppermute(at_chip, "core", perm=swap)
    own_half = expert_apply(at_chip, expert_in, expert_out)
    own_half, partner_rows = lax.optimization_barrier((own_half, partner_rows))
    partner_half = expert_apply(partner_rows, expert_in, expert_out)
    other_half = lax.ppermute(partner_half.astype(jnp.bfloat16), "core", perm=swap)
    summed = (own_half + other_half.astype(jnp.float32)).astype(jnp.bfloat16)
    returned = lax.all_to_all(summed, CHIPS, split_axis=0, concat_axis=0, tiled=True)
    summed_rows = returned.reshape(experts * capacity, width)
    picked_rows = jnp.take(summed_rows, slot_of, axis=0)
    weighted = picked_rows.astype(jnp.float32) * gate_weights.reshape(-1)[:, None]
    expert_sum = jnp.sum(weighted.reshape(tok_dev, TOPK, width), axis=1)
    return (residual + expert_sum).astype(jnp.bfloat16)


def solution(mesh):
    placed = (
        P(WN, None),
        P(WN, None),
        P(WN, None),
        P("wide", NARROW, None),
        P("wide", None),
        P("wide", None),
        P("wide", None, None),
        P(),
        P(),
        P(),
        P(WN, None),
        P(WN, None),
        P(WN, None, None),
        P(WN, None, None),
    )
    mesh = Mesh(mesh.devices.reshape(mesh.shape["wide"], -1, 2), ("wide", "y", "core"))
    return jax.shard_map(
        shards, mesh=mesh, in_specs=placed, out_specs=P(WN, None), check_vma=False
    )
```

```python
import functools

import jax
import jax.numpy as jnp
from jax import lax
from jax.experimental import pallas as pl
from jax.experimental.pallas import tpu as pltpu
from jax.sharding import Mesh
from jax.sharding import PartitionSpec as P

QH = 16
KVH = 4
HD = 128
TOPK = 6
PAGE_CAP = 2
NARROW = ("y", "core")
CHIPS = ("wide", "y")
WN = ("wide", "y", "core")


norm_eps = 1e-06
block_limit = 512
BQ = 128
BK = 128
LANES = 128


def rank_among_equal(values):
    length = values.shape[0]
    order = jnp.arange(length, dtype=jnp.int32)
    earlier = (values[None, :] == values[:, None]) & (order[None, :] < order[:, None])
    return jnp.sum(earlier.astype(jnp.int32), axis=1)


def block_scores(q_block, keys):
    return jnp.einsum("bhd,kd->hbk", q_block, keys, preferred_element_type=jnp.float32) * HD ** (
        -0.5
    )


def fresh_scores(start_row, q_heads, key_new, seg_all, block_len):
    q_block = lax.dynamic_slice_in_dim(q_heads, start_row, block_len, 0)
    seg_block = lax.dynamic_slice_in_dim(seg_all, start_row, block_len, 0)
    row_pos = start_row + jnp.arange(block_len, dtype=jnp.int32)
    positions = jnp.arange(seg_all.shape[0], dtype=jnp.int32)
    visible = (seg_block[:, None] == seg_all[None, :]) & (positions[None, :] <= row_pos[:, None])
    scores = jnp.where(visible[None], block_scores(q_block, key_new), -jnp.inf)
    return (q_block, seg_block, scores)


def attend_masked(
    start_row,
    q_heads,
    key_new,
    value_new,
    key_cached,
    value_cached,
    seg_all,
    lengths,
    cache_max,
    block_len,
):
    q_block, seg_block, fresh = fresh_scores(start_row, q_heads, key_new, seg_all, block_len)
    key_req = jnp.arange(key_cached.shape[0], dtype=jnp.int32) // cache_max
    key_pos = jnp.arange(key_cached.shape[0], dtype=jnp.int32) % cache_max
    visible = (seg_block[:, None] == key_req[None, :]) & (
        key_pos[None, :] < lengths[key_req][None, :]
    )
    older = jnp.where(visible[None], block_scores(q_block, key_cached), -jnp.inf)
    row_max = jnp.maximum(jnp.max(fresh, axis=-1), jnp.max(older, axis=-1))
    fresh_exp = jnp.exp(fresh - row_max[..., None])
    older_exp = jnp.exp(older - row_max[..., None])
    row_total = jnp.sum(fresh_exp, axis=-1) + jnp.sum(older_exp, axis=-1)
    fresh_w = (fresh_exp / row_total[..., None]).astype(jnp.bfloat16)
    older_w = (older_exp / row_total[..., None]).astype(jnp.bfloat16)
    attended = jnp.einsum("hbk,kd->bhd", fresh_w, value_new, preferred_element_type=jnp.float32)
    attended = attended + jnp.einsum(
        "hbk,kd->bhd", older_w, value_cached, preferred_element_type=jnp.float32
    )
    return attended.astype(jnp.bfloat16).reshape(block_len, -1)


def slot_attention(q_rows, kv_new, kv_cached, seg_all, lengths, cache_max):
    tokens = q_rows.shape[0]
    slots = lengths.shape[0]
    scale = HD ** (-0.5)
    n_q = tokens // BQ
    new_steps = (cache_max + BQ) // BK
    steps = new_steps + slots
    seg_start = jnp.sum(
        (seg_all[None, :] < jnp.arange(slots, dtype=jnp.int32)[:, None]).astype(jnp.int32), axis=1
    )
    firsts = seg_all[::BQ]
    lasts = seg_all[BQ - 1 :: BQ]
    kb_hi = (jnp.arange(n_q, dtype=jnp.int32) * BQ + BQ - 1) // BK
    kb_lo = jnp.maximum(seg_start[firsts] // BK, kb_hi - (new_steps - 1))
    n_new = kb_hi - kb_lo + 1
    n_old = lasts - firsts + 1
    t = jnp.arange(steps, dtype=jnp.int32)[None, :]
    new_idx = (kb_lo[:, None] + jnp.minimum(t, n_new[:, None] - 1)).reshape(-1)
    old_idx = (firsts[:, None] + jnp.clip(t - n_new[:, None], 0, n_old[:, None] - 1)).reshape(-1)
    counts = jnp.stack([n_new, n_old], axis=1).reshape(-1)
    q2 = q_rows.reshape(n_q, BQ, 2, HD).transpose(0, 2, 1, 3).reshape(n_q, 2 * BQ, HD)
    seg_q = jnp.broadcast_to(seg_all.reshape(n_q, 1, BQ, 1), (n_q, 2, BQ, LANES)).reshape(n_q, 2 * BQ, LANES)
    seg_k = jnp.broadcast_to(seg_all.reshape(tokens // BK, 1, BK), (tokens // BK, 8, BK))
    cached = kv_cached.reshape(slots, cache_max, 2 * HD)

    def kernel(new_sm, old_sm, cnt_sm, len_sm, q_ref, segq_ref, kn_ref, vn_ref, segk_ref, kc_ref, vc_ref, o_ref,
               m_ref, l_ref, acc_ref):
        b = pl.program_id(0)
        step = pl.program_id(1)
        nn = cnt_sm[2 * b]
        no = cnt_sm[2 * b + 1]

        @pl.when(step == 0)
        def _():
            m_ref[...] = jnp.full(m_ref.shape, -1e30, jnp.float32)
            l_ref[...] = jnp.zeros(l_ref.shape, jnp.float32)
            acc_ref[...] = jnp.zeros(acc_ref.shape, jnp.float32)

        def widen(x, width):
            return x if width == LANES else jnp.concatenate([x] * (width // LANES), axis=1)

        def visit(s, v):
            m = m_ref[...]
            m_new = jnp.maximum(m, jnp.max(s, axis=1, keepdims=True))
            alpha = jnp.exp(m - m_new)
            p = jnp.exp(s - widen(m_new, s.shape[1]))
            l_ref[...] = l_ref[...] * alpha + jnp.sum(p, axis=1, keepdims=True)
            acc_ref[...] = acc_ref[...] * alpha + jnp.dot(
                p.astype(jnp.bfloat16), v, preferred_element_type=jnp.float32)
            m_ref[...] = m_new

        q = q_ref[0]
        sq = segq_ref[0]

        @pl.when(step < nn)
        def _():
            kb = new_sm[b * steps + step]
            s = lax.dot_general(q, kn_ref[...], (((1,), (1,)), ((), ())),
                                preferred_element_type=jnp.float32) * scale
            rows = lax.broadcasted_iota(jnp.int32, s.shape, 0)
            cols = lax.broadcasted_iota(jnp.int32, s.shape, 1)
            qpos = b * BQ + jnp.bitwise_and(rows, BQ - 1)
            vis = (sq == segk_ref[0][:1, :]) & (kb * BK + cols <= qpos)
            visit(jnp.where(vis, s, -jnp.inf), vn_ref[...])

        @pl.when((step >= nn) & (step < nn + no))
        def _():
            r = old_sm[b * steps + step]
            s = lax.dot_general(q, kc_ref[0], (((1,), (1,)), ((), ())),
                                preferred_element_type=jnp.float32) * scale
            cols = lax.broadcasted_iota(jnp.int32, s.shape, 1)
            vis = (widen(sq, s.shape[1]) == r) & (cols < len_sm[r])
            visit(jnp.where(vis, s, -jnp.inf), vc_ref[0])

        @pl.when(step == steps - 1)
        def _():
            o_ref[0] = (acc_ref[...] / l_ref[...]).astype(jnp.bfloat16)

    def at(table):
        return lambda b, t, new_sm, old_sm, cnt_sm, len_sm: table(b, t, new_sm, old_sm)

    grid_spec = pltpu.PrefetchScalarGridSpec(
        num_scalar_prefetch=4,
        grid=(n_q, steps),
        in_specs=[
            pl.BlockSpec((1, 2 * BQ, HD), lambda b, t2, *_: (b, 0, 0)),
            pl.BlockSpec((1, 2 * BQ, LANES), lambda b, t2, *_: (b, 0, 0)),
            pl.BlockSpec((BK, HD), at(lambda b, t, n, o: (n[b * steps + t], 0))),
            pl.BlockSpec((BK, HD), at(lambda b, t, n, o: (n[b * steps + t], 1))),
            pl.BlockSpec((1, 8, BK), at(lambda b, t, n, o: (n[b * steps + t], 0, 0))),
            pl.BlockSpec((1, cache_max, HD), at(lambda b, t, n, o: (o[b * steps + t], 0, 0))),
            pl.BlockSpec((1, cache_max, HD), at(lambda b, t, n, o: (o[b * steps + t], 0, 1))),
        ],
        out_specs=pl.BlockSpec((1, 2 * BQ, HD), lambda b, t2, *_: (b, 0, 0)),
        scratch_shapes=[
            pltpu.VMEM((2 * BQ, LANES), jnp.float32),
            pltpu.VMEM((2 * BQ, LANES), jnp.float32),
            pltpu.VMEM((2 * BQ, HD), jnp.float32),
        ],
    )
    out = pl.pallas_call(
        kernel,
        grid_spec=grid_spec,
        out_shape=jax.ShapeDtypeStruct((n_q, 2 * BQ, HD), jnp.bfloat16),
    )(new_idx, old_idx, counts, lengths, q2, seg_q, kv_new, kv_new, seg_k, cached, cached)
    return out.reshape(n_q, 2, BQ, HD).transpose(0, 2, 1, 3).reshape(tokens, 2 * HD)


def expert_apply(rows_in, expert_in, expert_out):
    dims_in = rows_in.shape
    flat = rows_in.reshape(-1, dims_in[-1])
    both = jnp.dot(flat, expert_in[0], preferred_element_type=jnp.float32)
    half_units = both.shape[1] // 2
    hidden = (jax.nn.silu(both[:, :half_units]) * both[:, half_units:]).astype(jnp.bfloat16)
    half_out = jnp.dot(hidden, expert_out[0], preferred_element_type=jnp.float32)
    return half_out.reshape(dims_in)


def shards(
    tokens,
    queries,
    new_kv,
    page_pool,
    seg_ids,
    cache_len,
    page_table,
    moves,
    out_weight,
    norm_gain,
    expert_ids,
    gate_weights,
    expert_in,
    expert_out,
):
    n_wide = lax.axis_size("wide")
    n_narrow = lax.axis_size("y") * lax.axis_size("core")
    my_group = lax.axis_index("wide")
    tok_dev, width = tokens.shape
    group_tok = tok_dev * n_narrow
    requests = moves.shape[0]
    page_rows = page_pool.shape[1]
    kv_feat = page_pool.shape[2]
    pages_each = page_pool.shape[0] // requests
    heads_here = QH // n_narrow
    group_size = QH // KVH
    ranks = rank_among_equal(moves)
    offsets = jnp.arange(n_wide, dtype=jnp.int32)
    places = jnp.arange(PAGE_CAP, dtype=jnp.int32)
    slot_hits = (moves[None, None, :] == offsets[:, None, None]) & (
        ranks[None, None, :] == places[None, :, None]
    )
    picked = jnp.sum(slot_hits.astype(jnp.int32) * jnp.arange(requests, dtype=jnp.int32), axis=2)
    filled = jnp.any(slot_hits, axis=2)
    by_dest = (offsets - my_group) % n_wide
    picked = picked[by_dest]
    filled = filled[by_dest]
    blocks = page_pool.reshape(requests, pages_each * page_rows, kv_feat)
    outgoing = jnp.take(blocks, picked.reshape(-1), axis=0).reshape(
        n_wide, PAGE_CAP, pages_each * page_rows, kv_feat
    )
    outgoing = jnp.where(filled[:, :, None, None], outgoing, jnp.zeros((), outgoing.dtype))
    arrived = lax.all_to_all(outgoing, "wide", split_axis=0, concat_axis=0, tiled=True)
    sources = (my_group - moves) % n_wide
    first_page = (sources * PAGE_CAP + ranks) * pages_each
    page_index = (first_page[:, None] + page_table[0]).reshape(-1)
    arrived = arrived.reshape(n_wide * PAGE_CAP * pages_each, page_rows, kv_feat)
    cached = jnp.take(arrived, page_index, axis=0)
    kv_of_dest = jnp.arange(n_narrow, dtype=jnp.int32) * heads_here // group_size
    q_send = queries.reshape(1, tok_dev, n_narrow, heads_here * HD)
    kv_send = jnp.take(new_kv.reshape(tok_dev, KVH, 2 * HD), kv_of_dest, axis=1).reshape(
        1, tok_dev, n_narrow, 2 * HD
    )
    cache_send = jnp.take(
        cached.reshape(requests * pages_each, page_rows, KVH, 2 * HD), kv_of_dest, axis=2
    )
    q_heads, kv_heads, cache_heads = (
        lax.all_to_all(q_send, NARROW, split_axis=2, concat_axis=1, tiled=True),
        lax.all_to_all(kv_send, NARROW, split_axis=2, concat_axis=1, tiled=True),
        lax.all_to_all(cache_send, NARROW, split_axis=2, concat_axis=1, tiled=True),
    )
    q_heads = q_heads.reshape(group_tok, heads_here, HD)
    kv_heads = kv_heads.reshape(group_tok, 2 * HD)
    cache_max = pages_each * page_rows * n_narrow
    cache_heads = cache_heads.reshape(requests * cache_max, 2 * HD)
    key_new = kv_heads[:, :HD]
    value_new = kv_heads[:, HD:]
    key_cached = cache_heads[:, :HD]
    value_cached = cache_heads[:, HD:]
    seg_all = seg_ids[0]
    lengths = cache_len[0]
    attended = slot_attention(
        q_heads.reshape(group_tok, heads_here * HD), kv_heads, cache_heads, seg_all, lengths, cache_max
    ).reshape(n_narrow, tok_dev, heads_here * HD)
    back_home = lax.all_to_all(attended, NARROW, split_axis=0, concat_axis=2, tiled=True)
    mixed = back_home.reshape(tok_dev, QH * HD)
    residual = tokens.astype(jnp.float32) + jnp.dot(
        mixed, out_weight, preferred_element_type=jnp.float32
    )
    scale_row = lax.rsqrt(jnp.mean(residual * residual, axis=-1, keepdims=True) + norm_eps)
    normed = (residual * scale_row * norm_gain).astype(jnp.bfloat16)
    experts = n_wide * n_narrow // 2
    capacity = tok_dev * TOPK * 4 // (3 * experts)
    flat_ids = expert_ids.reshape(-1)
    onehot = (flat_ids[:, None] == jnp.arange(experts, dtype=jnp.int32)[None, :]).astype(jnp.int32)
    before = jnp.cumsum(onehot, axis=0) - onehot
    slot_place = jnp.sum(before * onehot, axis=1)
    slot_of = flat_ids * capacity + slot_place
    token_of = jnp.arange(tok_dev * TOPK, dtype=jnp.int32) // TOPK
    slot_token = jnp.zeros((experts * capacity,), jnp.int32).at[slot_of].set(token_of)
    slot_used = jnp.zeros((experts * capacity,), jnp.bool_).at[slot_of].set(True)
    outgoing_rows = jnp.where(
        slot_used[:, None], jnp.take(normed, slot_token, axis=0), jnp.zeros((), jnp.bfloat16)
    )
    outgoing_rows = outgoing_rows.reshape(experts, capacity, width)
    at_chip = lax.all_to_all(outgoing_rows, CHIPS, split_axis=0, concat_axis=0, tiled=True)
    swap = [(0, 1), (1, 0)]
    half_cap = capacity // 2
    partner_rows = lax.ppermute(at_chip, "core", perm=swap)
    own_first = expert_apply(at_chip[:, :half_cap], expert_in, expert_out)
    own_first, partner_rows = lax.optimization_barrier((own_first, partner_rows))
    partner_first = expert_apply(partner_rows[:, :half_cap], expert_in, expert_out)
    other_first = lax.ppermute(partner_first.astype(jnp.bfloat16), "core", perm=swap)
    own_second = expert_apply(at_chip[:, half_cap:], expert_in, expert_out)
    own_second, other_first = lax.optimization_barrier((own_second, other_first))
    summed_first = (own_first + other_first.astype(jnp.float32)).astype(jnp.bfloat16)
    back_first = lax.all_to_all(summed_first, CHIPS, split_axis=0, concat_axis=0, tiled=True)
    partner_second = expert_apply(partner_rows[:, half_cap:], expert_in, expert_out)
    partner_second, back_first = lax.optimization_barrier((partner_second, back_first))
    other_second = lax.ppermute(partner_second.astype(jnp.bfloat16), "core", perm=swap)
    summed_second = (own_second + other_second.astype(jnp.float32)).astype(jnp.bfloat16)
    back_second = lax.all_to_all(summed_second, CHIPS, split_axis=0, concat_axis=0, tiled=True)
    returned = jnp.concatenate([back_first, back_second], axis=1)
    summed_rows = returned.reshape(experts * capacity, width)
    picked_rows = jnp.take(summed_rows, slot_of, axis=0)
    weighted = picked_rows.astype(jnp.float32) * gate_weights.reshape(-1)[:, None]
    expert_sum = jnp.sum(weighted.reshape(tok_dev, TOPK, width), axis=1)
    return (residual + expert_sum).astype(jnp.bfloat16)


def solution(mesh):
    placed = (
        P(WN, None),
        P(WN, None),
        P(WN, None),
        P("wide", NARROW, None),
        P("wide", None),
        P("wide", None),
        P("wide", None, None),
        P(),
        P(),
        P(),
        P(WN, None),
        P(WN, None),
        P(WN, None, None),
        P(WN, None, None),
    )
    mesh = Mesh(mesh.devices.reshape(mesh.shape["wide"], -1, 2), ("wide", "y", "core"))
    return jax.shard_map(
        shards, mesh=mesh, in_specs=placed, out_specs=P(WN, None), check_vma=False
    )
```

```python
import functools

import jax
import jax.numpy as jnp
from jax import lax
from jax.experimental import pallas as pl
from jax.experimental.pallas import tpu as pltpu
from jax.sharding import Mesh
from jax.sharding import PartitionSpec as P

QH = 16
KVH = 4
HD = 128
TOPK = 6
PAGE_CAP = 2
NARROW = ("y", "core")
CHIPS = ("wide", "y")
WN = ("wide", "y", "core")


norm_eps = 1e-06
block_limit = 512
BQ = 128
BK = 128
LANES = 128


def rank_among_equal(values):
    length = values.shape[0]
    order = jnp.arange(length, dtype=jnp.int32)
    earlier = (values[None, :] == values[:, None]) & (order[None, :] < order[:, None])
    return jnp.sum(earlier.astype(jnp.int32), axis=1)


def block_scores(q_block, keys):
    return jnp.einsum("bhd,kd->hbk", q_block, keys, preferred_element_type=jnp.float32) * HD ** (
        -0.5
    )


def fresh_scores(start_row, q_heads, key_new, seg_all, block_len):
    q_block = lax.dynamic_slice_in_dim(q_heads, start_row, block_len, 0)
    seg_block = lax.dynamic_slice_in_dim(seg_all, start_row, block_len, 0)
    row_pos = start_row + jnp.arange(block_len, dtype=jnp.int32)
    positions = jnp.arange(seg_all.shape[0], dtype=jnp.int32)
    visible = (seg_block[:, None] == seg_all[None, :]) & (positions[None, :] <= row_pos[:, None])
    scores = jnp.where(visible[None], block_scores(q_block, key_new), -jnp.inf)
    return (q_block, seg_block, scores)


def attend_masked(
    start_row,
    q_heads,
    key_new,
    value_new,
    key_cached,
    value_cached,
    seg_all,
    lengths,
    cache_max,
    block_len,
):
    q_block, seg_block, fresh = fresh_scores(start_row, q_heads, key_new, seg_all, block_len)
    key_req = jnp.arange(key_cached.shape[0], dtype=jnp.int32) // cache_max
    key_pos = jnp.arange(key_cached.shape[0], dtype=jnp.int32) % cache_max
    visible = (seg_block[:, None] == key_req[None, :]) & (
        key_pos[None, :] < lengths[key_req][None, :]
    )
    older = jnp.where(visible[None], block_scores(q_block, key_cached), -jnp.inf)
    row_max = jnp.maximum(jnp.max(fresh, axis=-1), jnp.max(older, axis=-1))
    fresh_exp = jnp.exp(fresh - row_max[..., None])
    older_exp = jnp.exp(older - row_max[..., None])
    row_total = jnp.sum(fresh_exp, axis=-1) + jnp.sum(older_exp, axis=-1)
    fresh_w = (fresh_exp / row_total[..., None]).astype(jnp.bfloat16)
    older_w = (older_exp / row_total[..., None]).astype(jnp.bfloat16)
    attended = jnp.einsum("hbk,kd->bhd", fresh_w, value_new, preferred_element_type=jnp.float32)
    attended = attended + jnp.einsum(
        "hbk,kd->bhd", older_w, value_cached, preferred_element_type=jnp.float32
    )
    return attended.astype(jnp.bfloat16).reshape(block_len, -1)


def slot_attention(q_rows, kv_new, kv_cached, seg_all, lengths, cache_max):
    tokens = q_rows.shape[0]
    slots = lengths.shape[0]
    scale = HD ** (-0.5)
    n_q = tokens // BQ
    new_steps = (cache_max + BQ) // BK
    steps = new_steps + slots
    seg_start = jnp.sum(
        (seg_all[None, :] < jnp.arange(slots, dtype=jnp.int32)[:, None]).astype(jnp.int32), axis=1
    )
    firsts = seg_all[::BQ]
    lasts = seg_all[BQ - 1 :: BQ]
    kb_hi = (jnp.arange(n_q, dtype=jnp.int32) * BQ + BQ - 1) // BK
    kb_lo = jnp.maximum(seg_start[firsts] // BK, kb_hi - (new_steps - 1))
    n_new = kb_hi - kb_lo + 1
    n_old = lasts - firsts + 1
    t = jnp.arange(steps, dtype=jnp.int32)[None, :]
    new_idx = (kb_lo[:, None] + jnp.minimum(t, n_new[:, None] - 1)).reshape(-1)
    old_idx = (firsts[:, None] + jnp.clip(t - n_new[:, None], 0, n_old[:, None] - 1)).reshape(-1)
    counts = jnp.stack([n_new, n_old], axis=1).reshape(-1)
    q2 = q_rows.reshape(n_q, BQ, 2, HD).transpose(0, 2, 1, 3).reshape(n_q, 2 * BQ, HD)
    seg_q = jnp.broadcast_to(seg_all.reshape(n_q, 1, BQ, 1), (n_q, 2, BQ, LANES)).reshape(n_q, 2 * BQ, LANES)
    seg_k = jnp.broadcast_to(seg_all.reshape(tokens // BK, 1, BK), (tokens // BK, 8, BK))
    cached = kv_cached.reshape(slots, cache_max, 2 * HD)

    def kernel(new_sm, old_sm, cnt_sm, len_sm, q_ref, segq_ref, kn_ref, vn_ref, segk_ref, kc_ref, vc_ref, o_ref,
               m_ref, l_ref, acc_ref):
        b = pl.program_id(0)
        step = pl.program_id(1)
        nn = cnt_sm[2 * b]
        no = cnt_sm[2 * b + 1]

        @pl.when(step == 0)
        def _():
            m_ref[...] = jnp.full(m_ref.shape, -1e30, jnp.float32)
            l_ref[...] = jnp.zeros(l_ref.shape, jnp.float32)
            acc_ref[...] = jnp.zeros(acc_ref.shape, jnp.float32)

        def widen(x, width):
            return x if width == LANES else jnp.concatenate([x] * (width // LANES), axis=1)

        def visit(s, v):
            m = m_ref[...]
            m_new = jnp.maximum(m, jnp.max(s, axis=1, keepdims=True))
            alpha = jnp.exp(m - m_new)
            p = jnp.exp(s - widen(m_new, s.shape[1]))
            l_ref[...] = l_ref[...] * alpha + jnp.sum(p, axis=1, keepdims=True)
            acc_ref[...] = acc_ref[...] * alpha + jnp.dot(
                p.astype(jnp.bfloat16), v, preferred_element_type=jnp.float32)
            m_ref[...] = m_new

        q = q_ref[0]
        sq = segq_ref[0]

        @pl.when(step < nn)
        def _():
            kb = new_sm[b * steps + step]
            s = lax.dot_general(q, kn_ref[...], (((1,), (1,)), ((), ())),
                                preferred_element_type=jnp.float32) * scale
            rows = lax.broadcasted_iota(jnp.int32, s.shape, 0)
            cols = lax.broadcasted_iota(jnp.int32, s.shape, 1)
            qpos = b * BQ + jnp.bitwise_and(rows, BQ - 1)
            vis = (sq == segk_ref[0][:1, :]) & (kb * BK + cols <= qpos)
            visit(jnp.where(vis, s, -jnp.inf), vn_ref[...])

        @pl.when((step >= nn) & (step < nn + no))
        def _():
            r = old_sm[b * steps + step]
            s = lax.dot_general(q, kc_ref[0], (((1,), (1,)), ((), ())),
                                preferred_element_type=jnp.float32) * scale
            cols = lax.broadcasted_iota(jnp.int32, s.shape, 1)
            vis = (widen(sq, s.shape[1]) == r) & (cols < len_sm[r])
            visit(jnp.where(vis, s, -jnp.inf), vc_ref[0])

        @pl.when(step == steps - 1)
        def _():
            o_ref[0] = (acc_ref[...] / l_ref[...]).astype(jnp.bfloat16)

    def at(table):
        return lambda b, t, new_sm, old_sm, cnt_sm, len_sm: table(b, t, new_sm, old_sm)

    grid_spec = pltpu.PrefetchScalarGridSpec(
        num_scalar_prefetch=4,
        grid=(n_q, steps),
        in_specs=[
            pl.BlockSpec((1, 2 * BQ, HD), lambda b, t2, *_: (b, 0, 0)),
            pl.BlockSpec((1, 2 * BQ, LANES), lambda b, t2, *_: (b, 0, 0)),
            pl.BlockSpec((BK, HD), at(lambda b, t, n, o: (n[b * steps + t], 0))),
            pl.BlockSpec((BK, HD), at(lambda b, t, n, o: (n[b * steps + t], 1))),
            pl.BlockSpec((1, 8, BK), at(lambda b, t, n, o: (n[b * steps + t], 0, 0))),
            pl.BlockSpec((1, cache_max, HD), at(lambda b, t, n, o: (o[b * steps + t], 0, 0))),
            pl.BlockSpec((1, cache_max, HD), at(lambda b, t, n, o: (o[b * steps + t], 0, 1))),
        ],
        out_specs=pl.BlockSpec((1, 2 * BQ, HD), lambda b, t2, *_: (b, 0, 0)),
        scratch_shapes=[
            pltpu.VMEM((2 * BQ, LANES), jnp.float32),
            pltpu.VMEM((2 * BQ, LANES), jnp.float32),
            pltpu.VMEM((2 * BQ, HD), jnp.float32),
        ],
    )
    out = pl.pallas_call(
        kernel,
        grid_spec=grid_spec,
        out_shape=jax.ShapeDtypeStruct((n_q, 2 * BQ, HD), jnp.bfloat16),
    )(new_idx, old_idx, counts, lengths, q2, seg_q, kv_new, kv_new, seg_k, cached, cached)
    return out.reshape(n_q, 2, BQ, HD).transpose(0, 2, 1, 3).reshape(tokens, 2 * HD)


def expert_apply(rows_in, expert_in, expert_out):
    dims_in = rows_in.shape
    flat = rows_in.reshape(-1, dims_in[-1])
    both = jnp.dot(flat, expert_in[0], preferred_element_type=jnp.float32)
    half_units = both.shape[1] // 2
    hidden = (jax.nn.silu(both[:, :half_units]) * both[:, half_units:]).astype(jnp.bfloat16)
    half_out = jnp.dot(hidden, expert_out[0], preferred_element_type=jnp.float32)
    return half_out.reshape(dims_in)


def shards(
    tokens,
    queries,
    new_kv,
    page_pool,
    seg_ids,
    cache_len,
    page_table,
    moves,
    out_weight,
    norm_gain,
    expert_ids,
    gate_weights,
    expert_in,
    expert_out,
):
    n_wide = lax.axis_size("wide")
    n_narrow = lax.axis_size("y") * lax.axis_size("core")
    my_group = lax.axis_index("wide")
    tok_dev, width = tokens.shape
    group_tok = tok_dev * n_narrow
    requests = moves.shape[0]
    page_rows = page_pool.shape[1]
    kv_feat = page_pool.shape[2]
    pages_each = page_pool.shape[0] // requests
    heads_here = QH // n_narrow
    group_size = QH // KVH
    ranks = rank_among_equal(moves)
    offsets = jnp.arange(n_wide, dtype=jnp.int32)
    places = jnp.arange(PAGE_CAP, dtype=jnp.int32)
    slot_hits = (moves[None, None, :] == offsets[:, None, None]) & (
        ranks[None, None, :] == places[None, :, None]
    )
    picked = jnp.sum(slot_hits.astype(jnp.int32) * jnp.arange(requests, dtype=jnp.int32), axis=2)
    filled = jnp.any(slot_hits, axis=2)
    by_dest = (offsets - my_group) % n_wide
    picked = picked[by_dest]
    filled = filled[by_dest]
    blocks = page_pool.reshape(requests, pages_each * page_rows, kv_feat)
    outgoing = jnp.take(blocks, picked.reshape(-1), axis=0).reshape(
        n_wide, PAGE_CAP, pages_each * page_rows, kv_feat
    )
    outgoing = jnp.where(filled[:, :, None, None], outgoing, jnp.zeros((), outgoing.dtype))
    arrived = lax.all_to_all(outgoing, "wide", split_axis=0, concat_axis=0, tiled=True)
    sources = (my_group - moves) % n_wide
    first_page = (sources * PAGE_CAP + ranks) * pages_each
    page_index = (first_page[:, None] + page_table[0]).reshape(-1)
    arrived = arrived.reshape(n_wide * PAGE_CAP * pages_each, page_rows, kv_feat)
    cached = jnp.take(arrived, page_index, axis=0)
    kv_of_dest = jnp.arange(n_narrow, dtype=jnp.int32) * heads_here // group_size
    q_send = queries.reshape(1, tok_dev, n_narrow, heads_here * HD)
    kv_send = jnp.take(new_kv.reshape(tok_dev, KVH, 2 * HD), kv_of_dest, axis=1).reshape(
        1, tok_dev, n_narrow, 2 * HD
    )
    cache_send = jnp.take(
        cached.reshape(requests * pages_each, page_rows, KVH, 2 * HD), kv_of_dest, axis=2
    )
    q_heads, kv_heads, cache_heads = (
        lax.all_to_all(q_send, NARROW, split_axis=2, concat_axis=1, tiled=True),
        lax.all_to_all(kv_send, NARROW, split_axis=2, concat_axis=1, tiled=True),
        lax.all_to_all(cache_send, NARROW, split_axis=2, concat_axis=1, tiled=True),
    )
    q_heads = q_heads.reshape(group_tok, heads_here, HD)
    kv_heads = kv_heads.reshape(group_tok, 2 * HD)
    cache_max = pages_each * page_rows * n_narrow
    cache_heads = cache_heads.reshape(requests * cache_max, 2 * HD)
    key_new = kv_heads[:, :HD]
    value_new = kv_heads[:, HD:]
    key_cached = cache_heads[:, :HD]
    value_cached = cache_heads[:, HD:]
    seg_all = seg_ids[0]
    lengths = cache_len[0]
    attended = slot_attention(
        q_heads.reshape(group_tok, heads_here * HD), kv_heads, cache_heads, seg_all, lengths, cache_max
    ).reshape(n_narrow, tok_dev, heads_here * HD)
    back_home = lax.all_to_all(attended, NARROW, split_axis=0, concat_axis=2, tiled=True)
    mixed = back_home.reshape(tok_dev, QH * HD)
    residual = tokens.astype(jnp.float32) + jnp.dot(
        mixed, out_weight, preferred_element_type=jnp.float32
    )
    scale_row = lax.rsqrt(jnp.mean(residual * residual, axis=-1, keepdims=True) + norm_eps)
    normed = (residual * scale_row * norm_gain).astype(jnp.bfloat16)
    experts = n_wide * n_narrow // 2
    capacity = tok_dev * TOPK * 4 // (3 * experts)
    flat_ids = expert_ids.reshape(-1)
    onehot = (flat_ids[:, None] == jnp.arange(experts, dtype=jnp.int32)[None, :]).astype(jnp.int32)
    before = jnp.cumsum(onehot, axis=0) - onehot
    slot_place = jnp.sum(before * onehot, axis=1)
    slot_of = flat_ids * capacity + slot_place
    token_of = jnp.arange(tok_dev * TOPK, dtype=jnp.int32) // TOPK
    slot_token = jnp.zeros((experts * capacity,), jnp.int32).at[slot_of].set(token_of)
    slot_used = jnp.zeros((experts * capacity,), jnp.bool_).at[slot_of].set(True)
    outgoing_rows = jnp.where(
        slot_used[:, None], jnp.take(normed, slot_token, axis=0), jnp.zeros((), jnp.bfloat16)
    )
    outgoing_rows = outgoing_rows.reshape(experts, capacity, width)
    at_chip = lax.all_to_all(outgoing_rows, CHIPS, split_axis=0, concat_axis=0, tiled=True)
    swap = [(0, 1), (1, 0)]
    partner_rows = lax.ppermute(at_chip, "core", perm=swap)
    own_half = expert_apply(at_chip, expert_in, expert_out)
    own_half, partner_rows = lax.optimization_barrier((own_half, partner_rows))
    partner_half = expert_apply(partner_rows, expert_in, expert_out)
    other_half = lax.ppermute(partner_half.astype(jnp.bfloat16), "core", perm=swap)
    summed = (own_half + other_half.astype(jnp.float32)).astype(jnp.bfloat16)
    returned = lax.all_to_all(summed, CHIPS, split_axis=0, concat_axis=0, tiled=True)
    summed_rows = returned.reshape(experts * capacity, width)
    slot_hit = slot_of[:, None] == jnp.arange(experts * capacity, dtype=jnp.int32)[None, :]
    gate_at = jnp.where(slot_hit, gate_weights.reshape(-1)[:, None], jnp.float32(0.0))
    gate_at = jnp.sum(gate_at.reshape(tok_dev, TOPK, experts * capacity), axis=1)
    expert_sum = jnp.dot(
        gate_at,
        summed_rows.astype(jnp.float32),
        precision=lax.Precision.HIGHEST,
        preferred_element_type=jnp.float32,
    )
    return (residual + expert_sum).astype(jnp.bfloat16)


def solution(mesh):
    placed = (
        P(WN, None),
        P(WN, None),
        P(WN, None),
        P("wide", NARROW, None),
        P("wide", None),
        P("wide", None),
        P("wide", None, None),
        P(),
        P(),
        P(),
        P(WN, None),
        P(WN, None),
        P(WN, None, None),
        P(WN, None, None),
    )
    mesh = Mesh(mesh.devices.reshape(mesh.shape["wide"], -1, 2), ("wide", "y", "core"))
    return jax.shard_map(
        shards, mesh=mesh, in_specs=placed, out_specs=P(WN, None), check_vma=False
    )
```

```python
import functools

import jax
import jax.numpy as jnp
from jax import lax
from jax.experimental import pallas as pl
from jax.experimental.pallas import tpu as pltpu
from jax.sharding import Mesh
from jax.sharding import PartitionSpec as P

QH = 16
KVH = 4
HD = 128
TOPK = 6
PAGE_CAP = 2
NARROW = ("y", "core")
CHIPS = ("wide", "y")
WN = ("wide", "y", "core")


norm_eps = 1e-06
block_limit = 512
BQ = 128
BK = 128
LANES = 128


def rank_among_equal(values):
    length = values.shape[0]
    order = jnp.arange(length, dtype=jnp.int32)
    earlier = (values[None, :] == values[:, None]) & (order[None, :] < order[:, None])
    return jnp.sum(earlier.astype(jnp.int32), axis=1)


def block_scores(q_block, keys):
    return jnp.einsum("bhd,kd->hbk", q_block, keys, preferred_element_type=jnp.float32) * HD ** (
        -0.5
    )


def fresh_scores(start_row, q_heads, key_new, seg_all, block_len):
    q_block = lax.dynamic_slice_in_dim(q_heads, start_row, block_len, 0)
    seg_block = lax.dynamic_slice_in_dim(seg_all, start_row, block_len, 0)
    row_pos = start_row + jnp.arange(block_len, dtype=jnp.int32)
    positions = jnp.arange(seg_all.shape[0], dtype=jnp.int32)
    visible = (seg_block[:, None] == seg_all[None, :]) & (positions[None, :] <= row_pos[:, None])
    scores = jnp.where(visible[None], block_scores(q_block, key_new), -jnp.inf)
    return (q_block, seg_block, scores)


def attend_masked(
    start_row,
    q_heads,
    key_new,
    value_new,
    key_cached,
    value_cached,
    seg_all,
    lengths,
    cache_max,
    block_len,
):
    q_block, seg_block, fresh = fresh_scores(start_row, q_heads, key_new, seg_all, block_len)
    key_req = jnp.arange(key_cached.shape[0], dtype=jnp.int32) // cache_max
    key_pos = jnp.arange(key_cached.shape[0], dtype=jnp.int32) % cache_max
    visible = (seg_block[:, None] == key_req[None, :]) & (
        key_pos[None, :] < lengths[key_req][None, :]
    )
    older = jnp.where(visible[None], block_scores(q_block, key_cached), -jnp.inf)
    row_max = jnp.maximum(jnp.max(fresh, axis=-1), jnp.max(older, axis=-1))
    fresh_exp = jnp.exp(fresh - row_max[..., None])
    older_exp = jnp.exp(older - row_max[..., None])
    row_total = jnp.sum(fresh_exp, axis=-1) + jnp.sum(older_exp, axis=-1)
    fresh_w = (fresh_exp / row_total[..., None]).astype(jnp.bfloat16)
    older_w = (older_exp / row_total[..., None]).astype(jnp.bfloat16)
    attended = jnp.einsum("hbk,kd->bhd", fresh_w, value_new, preferred_element_type=jnp.float32)
    attended = attended + jnp.einsum(
        "hbk,kd->bhd", older_w, value_cached, preferred_element_type=jnp.float32
    )
    return attended.astype(jnp.bfloat16).reshape(block_len, -1)


def slot_attention(q_rows, kv_new, kv_cached, seg_all, lengths, cache_max):
    tokens = q_rows.shape[0]
    slots = lengths.shape[0]
    scale = HD ** (-0.5)
    n_q = tokens // BQ
    new_steps = (cache_max + BQ) // BK
    steps = new_steps + slots
    seg_start = jnp.sum(
        (seg_all[None, :] < jnp.arange(slots, dtype=jnp.int32)[:, None]).astype(jnp.int32), axis=1
    )
    firsts = seg_all[::BQ]
    lasts = seg_all[BQ - 1 :: BQ]
    kb_hi = (jnp.arange(n_q, dtype=jnp.int32) * BQ + BQ - 1) // BK
    kb_lo = jnp.maximum(seg_start[firsts] // BK, kb_hi - (new_steps - 1))
    n_new = kb_hi - kb_lo + 1
    n_old = lasts - firsts + 1
    t = jnp.arange(steps, dtype=jnp.int32)[None, :]
    new_idx = (kb_lo[:, None] + jnp.minimum(t, n_new[:, None] - 1)).reshape(-1)
    old_idx = (firsts[:, None] + jnp.clip(t - n_new[:, None], 0, n_old[:, None] - 1)).reshape(-1)
    counts = jnp.stack([n_new, n_old], axis=1).reshape(-1)
    q2 = q_rows.reshape(n_q, BQ, 2, HD).transpose(0, 2, 1, 3).reshape(n_q, 2 * BQ, HD)
    seg_q = jnp.broadcast_to(seg_all.reshape(n_q, 1, BQ, 1), (n_q, 2, BQ, LANES)).reshape(n_q, 2 * BQ, LANES)
    seg_k = jnp.broadcast_to(seg_all.reshape(tokens // BK, 1, BK), (tokens // BK, 8, BK))
    cached = kv_cached.reshape(slots, cache_max, 2 * HD)

    def kernel(new_sm, old_sm, cnt_sm, len_sm, q_ref, segq_ref, kn_ref, vn_ref, segk_ref, kc_ref, vc_ref, o_ref,
               m_ref, l_ref, acc_ref):
        b = pl.program_id(0)
        step = pl.program_id(1)
        nn = cnt_sm[2 * b]
        no = cnt_sm[2 * b + 1]

        @pl.when(step == 0)
        def _():
            m_ref[...] = jnp.full(m_ref.shape, -1e30, jnp.float32)
            l_ref[...] = jnp.zeros(l_ref.shape, jnp.float32)
            acc_ref[...] = jnp.zeros(acc_ref.shape, jnp.float32)

        def widen(x, width):
            return x if width == LANES else jnp.concatenate([x] * (width // LANES), axis=1)

        def visit(s, v):
            m = m_ref[...]
            m_new = jnp.maximum(m, jnp.max(s, axis=1, keepdims=True))
            alpha = jnp.exp(m - m_new)
            p = jnp.exp(s - widen(m_new, s.shape[1]))
            l_ref[...] = l_ref[...] * alpha + jnp.sum(p, axis=1, keepdims=True)
            acc_ref[...] = acc_ref[...] * alpha + jnp.dot(
                p.astype(jnp.bfloat16), v, preferred_element_type=jnp.float32)
            m_ref[...] = m_new

        q = q_ref[0]
        sq = segq_ref[0]

        @pl.when(step < nn)
        def _():
            kb = new_sm[b * steps + step]
            s = lax.dot_general(q, kn_ref[...], (((1,), (1,)), ((), ())),
                                preferred_element_type=jnp.float32) * scale
            rows = lax.broadcasted_iota(jnp.int32, s.shape, 0)
            cols = lax.broadcasted_iota(jnp.int32, s.shape, 1)
            qpos = b * BQ + jnp.bitwise_and(rows, BQ - 1)
            vis = (sq == segk_ref[0][:1, :]) & (kb * BK + cols <= qpos)
            visit(jnp.where(vis, s, -jnp.inf), vn_ref[...])

        @pl.when((step >= nn) & (step < nn + no))
        def _():
            r = old_sm[b * steps + step]
            s = lax.dot_general(q, kc_ref[0], (((1,), (1,)), ((), ())),
                                preferred_element_type=jnp.float32) * scale
            cols = lax.broadcasted_iota(jnp.int32, s.shape, 1)
            vis = (widen(sq, s.shape[1]) == r) & (cols < len_sm[r])
            visit(jnp.where(vis, s, -jnp.inf), vc_ref[0])

        @pl.when(step == steps - 1)
        def _():
            o_ref[0] = (acc_ref[...] / l_ref[...]).astype(jnp.bfloat16)

    def at(table):
        return lambda b, t, new_sm, old_sm, cnt_sm, len_sm: table(b, t, new_sm, old_sm)

    grid_spec = pltpu.PrefetchScalarGridSpec(
        num_scalar_prefetch=4,
        grid=(n_q, steps),
        in_specs=[
            pl.BlockSpec((1, 2 * BQ, HD), lambda b, t2, *_: (b, 0, 0)),
            pl.BlockSpec((1, 2 * BQ, LANES), lambda b, t2, *_: (b, 0, 0)),
            pl.BlockSpec((BK, HD), at(lambda b, t, n, o: (n[b * steps + t], 0))),
            pl.BlockSpec((BK, HD), at(lambda b, t, n, o: (n[b * steps + t], 1))),
            pl.BlockSpec((1, 8, BK), at(lambda b, t, n, o: (n[b * steps + t], 0, 0))),
            pl.BlockSpec((1, cache_max, HD), at(lambda b, t, n, o: (o[b * steps + t], 0, 0))),
            pl.BlockSpec((1, cache_max, HD), at(lambda b, t, n, o: (o[b * steps + t], 0, 1))),
        ],
        out_specs=pl.BlockSpec((1, 2 * BQ, HD), lambda b, t2, *_: (b, 0, 0)),
        scratch_shapes=[
            pltpu.VMEM((2 * BQ, LANES), jnp.float32),
            pltpu.VMEM((2 * BQ, LANES), jnp.float32),
            pltpu.VMEM((2 * BQ, HD), jnp.float32),
        ],
    )
    out = pl.pallas_call(
        kernel,
        grid_spec=grid_spec,
        out_shape=jax.ShapeDtypeStruct((n_q, 2 * BQ, HD), jnp.bfloat16),
    )(new_idx, old_idx, counts, lengths, q2, seg_q, kv_new, kv_new, seg_k, cached, cached)
    return out.reshape(n_q, 2, BQ, HD).transpose(0, 2, 1, 3).reshape(tokens, 2 * HD)


def expert_apply(rows_in, expert_in, expert_out):
    dims_in = rows_in.shape
    flat = rows_in.reshape(-1, dims_in[-1])
    both = jnp.dot(flat, expert_in[0], preferred_element_type=jnp.float32)
    half_units = both.shape[1] // 2
    hidden = (jax.nn.silu(both[:, :half_units]) * both[:, half_units:]).astype(jnp.bfloat16)
    half_out = jnp.dot(hidden, expert_out[0], preferred_element_type=jnp.float32)
    return half_out.reshape(dims_in)


def shards(
    tokens,
    queries,
    new_kv,
    page_pool,
    seg_ids,
    cache_len,
    page_table,
    moves,
    out_weight,
    norm_gain,
    expert_ids,
    gate_weights,
    expert_in,
    expert_out,
):
    n_wide = lax.axis_size("wide")
    n_narrow = lax.axis_size("y") * lax.axis_size("core")
    my_group = lax.axis_index("wide")
    tok_dev, width = tokens.shape
    group_tok = tok_dev * n_narrow
    requests = moves.shape[0]
    page_rows = page_pool.shape[1]
    kv_feat = page_pool.shape[2]
    pages_each = page_pool.shape[0] // requests
    heads_here = QH // n_narrow
    group_size = QH // KVH
    ranks = rank_among_equal(moves)
    offsets = jnp.arange(n_wide, dtype=jnp.int32)
    places = jnp.arange(PAGE_CAP, dtype=jnp.int32)
    slot_hits = (moves[None, None, :] == offsets[:, None, None]) & (
        ranks[None, None, :] == places[None, :, None]
    )
    picked = jnp.sum(slot_hits.astype(jnp.int32) * jnp.arange(requests, dtype=jnp.int32), axis=2)
    filled = jnp.any(slot_hits, axis=2)
    by_dest = (offsets - my_group) % n_wide
    picked = picked[by_dest]
    filled = filled[by_dest]
    blocks = page_pool.reshape(requests, pages_each * page_rows, kv_feat)
    outgoing = jnp.take(blocks, picked.reshape(-1), axis=0).reshape(
        n_wide, PAGE_CAP, pages_each * page_rows, kv_feat
    )
    outgoing = jnp.where(filled[:, :, None, None], outgoing, jnp.zeros((), outgoing.dtype))
    arrived = lax.all_to_all(outgoing, "wide", split_axis=0, concat_axis=0, tiled=True)
    sources = (my_group - moves) % n_wide
    first_page = (sources * PAGE_CAP + ranks) * pages_each
    page_index = (first_page[:, None] + page_table[0]).reshape(-1)
    arrived = arrived.reshape(n_wide * PAGE_CAP * pages_each, page_rows, kv_feat)
    cached = jnp.take(arrived, page_index, axis=0)
    kv_of_dest = jnp.arange(n_narrow, dtype=jnp.int32) * heads_here // group_size
    q_send = queries.reshape(1, tok_dev, n_narrow, heads_here * HD)
    kv_send = jnp.take(new_kv.reshape(tok_dev, KVH, 2 * HD), kv_of_dest, axis=1).reshape(
        1, tok_dev, n_narrow, 2 * HD
    )
    cache_send = jnp.take(
        cached.reshape(requests * pages_each, page_rows, KVH, 2 * HD), kv_of_dest, axis=2
    )
    q_heads, kv_heads, cache_heads = (
        lax.all_to_all(q_send, NARROW, split_axis=2, concat_axis=1, tiled=True),
        lax.all_to_all(kv_send, NARROW, split_axis=2, concat_axis=1, tiled=True),
        lax.all_to_all(cache_send, NARROW, split_axis=2, concat_axis=1, tiled=True),
    )
    q_heads = q_heads.reshape(group_tok, heads_here, HD)
    kv_heads = kv_heads.reshape(group_tok, 2 * HD)
    cache_max = pages_each * page_rows * n_narrow
    cache_heads = cache_heads.reshape(requests * cache_max, 2 * HD)
    key_new = kv_heads[:, :HD]
    value_new = kv_heads[:, HD:]
    key_cached = cache_heads[:, :HD]
    value_cached = cache_heads[:, HD:]
    seg_all = seg_ids[0]
    lengths = cache_len[0]
    attended = slot_attention(
        q_heads.reshape(group_tok, heads_here * HD), kv_heads, cache_heads, seg_all, lengths, cache_max
    ).reshape(n_narrow, tok_dev, heads_here * HD)
    back_home = lax.all_to_all(attended, NARROW, split_axis=0, concat_axis=2, tiled=True)
    mixed = back_home.reshape(tok_dev, QH * HD)
    residual = tokens.astype(jnp.float32) + jnp.dot(
        mixed, out_weight, preferred_element_type=jnp.float32
    )
    scale_row = lax.rsqrt(jnp.mean(residual * residual, axis=-1, keepdims=True) + norm_eps)
    normed = (residual * scale_row * norm_gain).astype(jnp.bfloat16)
    experts = n_wide * n_narrow // 2
    capacity = tok_dev * TOPK * 4 // (3 * experts)
    flat_ids = expert_ids.reshape(-1)
    onehot = (flat_ids[:, None] == jnp.arange(experts, dtype=jnp.int32)[None, :]).astype(jnp.int32)
    before = jnp.cumsum(onehot, axis=0) - onehot
    slot_place = jnp.sum(before * onehot, axis=1)
    slot_of = flat_ids * capacity + slot_place
    slot_hit = slot_of[None, :] == jnp.arange(experts * capacity, dtype=jnp.int32)[:, None]
    pick = jnp.any(slot_hit.reshape(experts * capacity, tok_dev, TOPK), axis=2).astype(jnp.bfloat16)
    outgoing_rows = jnp.dot(pick, normed, preferred_element_type=jnp.float32).astype(jnp.bfloat16)
    outgoing_rows = outgoing_rows.reshape(experts, capacity, width)
    at_chip = lax.all_to_all(outgoing_rows, CHIPS, split_axis=0, concat_axis=0, tiled=True)
    swap = [(0, 1), (1, 0)]
    partner_rows = lax.ppermute(at_chip, "core", perm=swap)
    own_half = expert_apply(at_chip, expert_in, expert_out)
    own_half, partner_rows = lax.optimization_barrier((own_half, partner_rows))
    partner_half = expert_apply(partner_rows, expert_in, expert_out)
    other_half = lax.ppermute(partner_half.astype(jnp.bfloat16), "core", perm=swap)
    summed = (own_half + other_half.astype(jnp.float32)).astype(jnp.bfloat16)
    returned = lax.all_to_all(summed, CHIPS, split_axis=0, concat_axis=0, tiled=True)
    summed_rows = returned.reshape(experts * capacity, width)
    gate_at = jnp.where(slot_hit.T, gate_weights.reshape(-1)[:, None], jnp.float32(0.0))
    gate_at = jnp.sum(gate_at.reshape(tok_dev, TOPK, experts * capacity), axis=1)
    expert_sum = jnp.dot(
        gate_at,
        summed_rows.astype(jnp.float32),
        precision=lax.Precision.HIGHEST,
        preferred_element_type=jnp.float32,
    )
    return (residual + expert_sum).astype(jnp.bfloat16)


def solution(mesh):
    placed = (
        P(WN, None),
        P(WN, None),
        P(WN, None),
        P("wide", NARROW, None),
        P("wide", None),
        P("wide", None),
        P("wide", None, None),
        P(),
        P(),
        P(),
        P(WN, None),
        P(WN, None),
        P(WN, None, None),
        P(WN, None, None),
    )
    mesh = Mesh(mesh.devices.reshape(mesh.shape["wide"], -1, 2), ("wide", "y", "core"))
    return jax.shard_map(
        shards, mesh=mesh, in_specs=placed, out_specs=P(WN, None), check_vma=False
    )
```

```python
import functools

import jax
import jax.numpy as jnp
from jax import lax
from jax.experimental import pallas as pl
from jax.experimental.pallas import tpu as pltpu
from jax.sharding import Mesh
from jax.sharding import PartitionSpec as P

QH = 16
KVH = 4
HD = 128
TOPK = 6
PAGE_CAP = 2
NARROW = ("y", "core")
CHIPS = ("wide", "y")
WN = ("wide", "y", "core")


norm_eps = 1e-06
block_limit = 512
BQ = 128
BK = 128
LANES = 128


def rank_among_equal(values):
    length = values.shape[0]
    order = jnp.arange(length, dtype=jnp.int32)
    earlier = (values[None, :] == values[:, None]) & (order[None, :] < order[:, None])
    return jnp.sum(earlier.astype(jnp.int32), axis=1)


def block_scores(q_block, keys):
    return jnp.einsum("bhd,kd->hbk", q_block, keys, preferred_element_type=jnp.float32) * HD ** (
        -0.5
    )


def fresh_scores(start_row, q_heads, key_new, seg_all, block_len):
    q_block = lax.dynamic_slice_in_dim(q_heads, start_row, block_len, 0)
    seg_block = lax.dynamic_slice_in_dim(seg_all, start_row, block_len, 0)
    row_pos = start_row + jnp.arange(block_len, dtype=jnp.int32)
    positions = jnp.arange(seg_all.shape[0], dtype=jnp.int32)
    visible = (seg_block[:, None] == seg_all[None, :]) & (positions[None, :] <= row_pos[:, None])
    scores = jnp.where(visible[None], block_scores(q_block, key_new), -jnp.inf)
    return (q_block, seg_block, scores)


def attend_masked(
    start_row,
    q_heads,
    key_new,
    value_new,
    key_cached,
    value_cached,
    seg_all,
    lengths,
    cache_max,
    block_len,
):
    q_block, seg_block, fresh = fresh_scores(start_row, q_heads, key_new, seg_all, block_len)
    key_req = jnp.arange(key_cached.shape[0], dtype=jnp.int32) // cache_max
    key_pos = jnp.arange(key_cached.shape[0], dtype=jnp.int32) % cache_max
    visible = (seg_block[:, None] == key_req[None, :]) & (
        key_pos[None, :] < lengths[key_req][None, :]
    )
    older = jnp.where(visible[None], block_scores(q_block, key_cached), -jnp.inf)
    row_max = jnp.maximum(jnp.max(fresh, axis=-1), jnp.max(older, axis=-1))
    fresh_exp = jnp.exp(fresh - row_max[..., None])
    older_exp = jnp.exp(older - row_max[..., None])
    row_total = jnp.sum(fresh_exp, axis=-1) + jnp.sum(older_exp, axis=-1)
    fresh_w = (fresh_exp / row_total[..., None]).astype(jnp.bfloat16)
    older_w = (older_exp / row_total[..., None]).astype(jnp.bfloat16)
    attended = jnp.einsum("hbk,kd->bhd", fresh_w, value_new, preferred_element_type=jnp.float32)
    attended = attended + jnp.einsum(
        "hbk,kd->bhd", older_w, value_cached, preferred_element_type=jnp.float32
    )
    return attended.astype(jnp.bfloat16).reshape(block_len, -1)


def slot_attention(q_rows, kv_new, kv_cached, seg_all, lengths, cache_max):
    tokens = q_rows.shape[0]
    slots = lengths.shape[0]
    scale = HD ** (-0.5)
    n_q = tokens // BQ
    new_steps = (cache_max + BQ) // BK
    steps = new_steps + slots
    seg_start = jnp.sum(
        (seg_all[None, :] < jnp.arange(slots, dtype=jnp.int32)[:, None]).astype(jnp.int32), axis=1
    )
    firsts = seg_all[::BQ]
    lasts = seg_all[BQ - 1 :: BQ]
    kb_hi = (jnp.arange(n_q, dtype=jnp.int32) * BQ + BQ - 1) // BK
    kb_lo = jnp.maximum(seg_start[firsts] // BK, kb_hi - (new_steps - 1))
    n_new = kb_hi - kb_lo + 1
    n_old = lasts - firsts + 1
    t = jnp.arange(steps, dtype=jnp.int32)[None, :]
    new_idx = (kb_lo[:, None] + jnp.minimum(t, n_new[:, None] - 1)).reshape(-1)
    old_idx = (firsts[:, None] + jnp.clip(t - n_new[:, None], 0, n_old[:, None] - 1)).reshape(-1)
    counts = jnp.stack([n_new, n_old], axis=1).reshape(-1)
    q2 = q_rows.reshape(n_q, BQ, 2, HD).transpose(0, 2, 1, 3).reshape(n_q, 2 * BQ, HD)
    seg_q = jnp.broadcast_to(seg_all.reshape(n_q, 1, BQ, 1), (n_q, 2, BQ, LANES)).reshape(n_q, 2 * BQ, LANES)
    seg_k = jnp.broadcast_to(seg_all.reshape(tokens // BK, 1, BK), (tokens // BK, 8, BK))
    cached = kv_cached.reshape(slots, cache_max, 2 * HD)

    def kernel(new_sm, old_sm, cnt_sm, len_sm, q_ref, segq_ref, kn_ref, vn_ref, segk_ref, kc_ref, vc_ref, o_ref,
               m_ref, l_ref, acc_ref):
        b = pl.program_id(0)
        step = pl.program_id(1)
        nn = cnt_sm[2 * b]
        no = cnt_sm[2 * b + 1]

        @pl.when(step == 0)
        def _():
            m_ref[...] = jnp.full(m_ref.shape, -1e30, jnp.float32)
            l_ref[...] = jnp.zeros(l_ref.shape, jnp.float32)
            acc_ref[...] = jnp.zeros(acc_ref.shape, jnp.float32)

        def widen(x, width):
            return x if width == LANES else jnp.concatenate([x] * (width // LANES), axis=1)

        def visit(s, v):
            m = m_ref[...]
            m_new = jnp.maximum(m, jnp.max(s, axis=1, keepdims=True))
            alpha = jnp.exp(m - m_new)
            p = jnp.exp(s - widen(m_new, s.shape[1]))
            l_ref[...] = l_ref[...] * alpha + jnp.sum(p, axis=1, keepdims=True)
            acc_ref[...] = acc_ref[...] * alpha + jnp.dot(
                p.astype(jnp.bfloat16), v, preferred_element_type=jnp.float32)
            m_ref[...] = m_new

        q = q_ref[0]
        sq = segq_ref[0]

        @pl.when(step < nn)
        def _():
            kb = new_sm[b * steps + step]
            s = lax.dot_general(q, kn_ref[...], (((1,), (1,)), ((), ())),
                                preferred_element_type=jnp.float32) * scale
            rows = lax.broadcasted_iota(jnp.int32, s.shape, 0)
            cols = lax.broadcasted_iota(jnp.int32, s.shape, 1)
            qpos = b * BQ + jnp.bitwise_and(rows, BQ - 1)
            vis = (sq == segk_ref[0][:1, :]) & (kb * BK + cols <= qpos)
            visit(jnp.where(vis, s, -jnp.inf), vn_ref[...])

        @pl.when((step >= nn) & (step < nn + no))
        def _():
            r = old_sm[b * steps + step]
            s = lax.dot_general(q, kc_ref[0], (((1,), (1,)), ((), ())),
                                preferred_element_type=jnp.float32) * scale
            cols = lax.broadcasted_iota(jnp.int32, s.shape, 1)
            vis = (widen(sq, s.shape[1]) == r) & (cols < len_sm[r])
            visit(jnp.where(vis, s, -jnp.inf), vc_ref[0])

        @pl.when(step == steps - 1)
        def _():
            o_ref[0] = (acc_ref[...] / l_ref[...]).astype(jnp.bfloat16)

    def at(table):
        return lambda b, t, new_sm, old_sm, cnt_sm, len_sm: table(b, t, new_sm, old_sm)

    grid_spec = pltpu.PrefetchScalarGridSpec(
        num_scalar_prefetch=4,
        grid=(n_q, steps),
        in_specs=[
            pl.BlockSpec((1, 2 * BQ, HD), lambda b, t2, *_: (b, 0, 0)),
            pl.BlockSpec((1, 2 * BQ, LANES), lambda b, t2, *_: (b, 0, 0)),
            pl.BlockSpec((BK, HD), at(lambda b, t, n, o: (n[b * steps + t], 0))),
            pl.BlockSpec((BK, HD), at(lambda b, t, n, o: (n[b * steps + t], 1))),
            pl.BlockSpec((1, 8, BK), at(lambda b, t, n, o: (n[b * steps + t], 0, 0))),
            pl.BlockSpec((1, cache_max, HD), at(lambda b, t, n, o: (o[b * steps + t], 0, 0))),
            pl.BlockSpec((1, cache_max, HD), at(lambda b, t, n, o: (o[b * steps + t], 0, 1))),
        ],
        out_specs=pl.BlockSpec((1, 2 * BQ, HD), lambda b, t2, *_: (b, 0, 0)),
        scratch_shapes=[
            pltpu.VMEM((2 * BQ, LANES), jnp.float32),
            pltpu.VMEM((2 * BQ, LANES), jnp.float32),
            pltpu.VMEM((2 * BQ, HD), jnp.float32),
        ],
    )
    out = pl.pallas_call(
        kernel,
        grid_spec=grid_spec,
        out_shape=jax.ShapeDtypeStruct((n_q, 2 * BQ, HD), jnp.bfloat16),
    )(new_idx, old_idx, counts, lengths, q2, seg_q, kv_new, kv_new, seg_k, cached, cached)
    return out.reshape(n_q, 2, BQ, HD).transpose(0, 2, 1, 3).reshape(tokens, 2 * HD)


def expert_apply(rows_in, expert_in, expert_out):
    dims_in = rows_in.shape
    flat = rows_in.reshape(-1, dims_in[-1])
    both = jnp.dot(flat, expert_in[0], preferred_element_type=jnp.float32)
    half_units = both.shape[1] // 2
    hidden = (jax.nn.silu(both[:, :half_units]) * both[:, half_units:]).astype(jnp.bfloat16)
    half_out = jnp.dot(hidden, expert_out[0], preferred_element_type=jnp.float32)
    return half_out.reshape(dims_in)


def shards(
    tokens,
    queries,
    new_kv,
    page_pool,
    seg_ids,
    cache_len,
    page_table,
    moves,
    out_weight,
    norm_gain,
    expert_ids,
    gate_weights,
    expert_in,
    expert_out,
):
    n_wide = lax.axis_size("wide")
    n_narrow = lax.axis_size("y") * lax.axis_size("core")
    my_group = lax.axis_index("wide")
    tok_dev, width = tokens.shape
    group_tok = tok_dev * n_narrow
    requests = moves.shape[0]
    page_rows = page_pool.shape[1]
    kv_feat = page_pool.shape[2]
    pages_each = page_pool.shape[0] // requests
    heads_here = QH // n_narrow
    group_size = QH // KVH
    ranks = rank_among_equal(moves)
    offsets = jnp.arange(n_wide, dtype=jnp.int32)
    places = jnp.arange(PAGE_CAP, dtype=jnp.int32)
    slot_hits = (moves[None, None, :] == offsets[:, None, None]) & (
        ranks[None, None, :] == places[None, :, None]
    )
    picked = jnp.sum(slot_hits.astype(jnp.int32) * jnp.arange(requests, dtype=jnp.int32), axis=2)
    by_dest = (offsets - my_group) % n_wide
    picked = picked[by_dest]
    blocks = page_pool.reshape(requests, pages_each * page_rows, kv_feat)
    outgoing = jnp.take(blocks, picked.reshape(-1), axis=0).reshape(
        n_wide, PAGE_CAP, pages_each * page_rows, kv_feat
    )
    arrived = lax.all_to_all(outgoing, "wide", split_axis=0, concat_axis=0, tiled=True)
    sources = (my_group - moves) % n_wide
    first_page = (sources * PAGE_CAP + ranks) * pages_each
    page_index = (first_page[:, None] + page_table[0]).reshape(-1)
    arrived = arrived.reshape(n_wide * PAGE_CAP * pages_each, page_rows, kv_feat)
    cached = jnp.take(arrived, page_index, axis=0)
    kv_of_dest = jnp.arange(n_narrow, dtype=jnp.int32) * heads_here // group_size
    q_send = queries.reshape(1, tok_dev, n_narrow, heads_here * HD)
    kv_send = jnp.take(new_kv.reshape(tok_dev, KVH, 2 * HD), kv_of_dest, axis=1).reshape(
        1, tok_dev, n_narrow, 2 * HD
    )
    cache_send = jnp.take(
        cached.reshape(requests * pages_each, page_rows, KVH, 2 * HD), kv_of_dest, axis=2
    )
    q_heads, kv_heads, cache_heads = (
        lax.all_to_all(q_send, NARROW, split_axis=2, concat_axis=1, tiled=True),
        lax.all_to_all(kv_send, NARROW, split_axis=2, concat_axis=1, tiled=True),
        lax.all_to_all(cache_send, NARROW, split_axis=2, concat_axis=1, tiled=True),
    )
    q_heads = q_heads.reshape(group_tok, heads_here, HD)
    kv_heads = kv_heads.reshape(group_tok, 2 * HD)
    cache_max = pages_each * page_rows * n_narrow
    cache_heads = cache_heads.reshape(requests * cache_max, 2 * HD)
    key_new = kv_heads[:, :HD]
    value_new = kv_heads[:, HD:]
    key_cached = cache_heads[:, :HD]
    value_cached = cache_heads[:, HD:]
    seg_all = seg_ids[0]
    lengths = cache_len[0]
    attended = slot_attention(
        q_heads.reshape(group_tok, heads_here * HD), kv_heads, cache_heads, seg_all, lengths, cache_max
    ).reshape(n_narrow, tok_dev, heads_here * HD)
    back_home = lax.all_to_all(attended, NARROW, split_axis=0, concat_axis=2, tiled=True)
    mixed = back_home.reshape(tok_dev, QH * HD)
    residual = tokens.astype(jnp.float32) + jnp.dot(
        mixed, out_weight, preferred_element_type=jnp.float32
    )
    scale_row = lax.rsqrt(jnp.mean(residual * residual, axis=-1, keepdims=True) + norm_eps)
    normed = (residual * scale_row * norm_gain).astype(jnp.bfloat16)
    experts = n_wide * n_narrow // 2
    capacity = tok_dev * TOPK * 4 // (3 * experts)
    flat_ids = expert_ids.reshape(-1)
    onehot = (flat_ids[:, None] == jnp.arange(experts, dtype=jnp.int32)[None, :]).astype(jnp.int32)
    before = jnp.cumsum(onehot, axis=0) - onehot
    slot_place = jnp.sum(before * onehot, axis=1)
    slot_of = flat_ids * capacity + slot_place
    slot_hit = slot_of[None, :] == jnp.arange(experts * capacity, dtype=jnp.int32)[:, None]
    pick = jnp.any(slot_hit.reshape(experts * capacity, tok_dev, TOPK), axis=2).astype(jnp.bfloat16)
    outgoing_rows = jnp.dot(pick, normed, preferred_element_type=jnp.float32).astype(jnp.bfloat16)
    outgoing_rows = outgoing_rows.reshape(experts, capacity, width)
    at_chip = lax.all_to_all(outgoing_rows, CHIPS, split_axis=0, concat_axis=0, tiled=True)
    swap = [(0, 1), (1, 0)]
    partner_rows = lax.ppermute(at_chip, "core", perm=swap)
    own_half = expert_apply(at_chip, expert_in, expert_out)
    own_half, partner_rows = lax.optimization_barrier((own_half, partner_rows))
    partner_half = expert_apply(partner_rows, expert_in, expert_out)
    other_half = lax.ppermute(partner_half.astype(jnp.bfloat16), "core", perm=swap)
    summed = (own_half + other_half.astype(jnp.float32)).astype(jnp.bfloat16)
    returned = lax.all_to_all(summed, CHIPS, split_axis=0, concat_axis=0, tiled=True)
    summed_rows = returned.reshape(experts * capacity, width)
    gate_at = jnp.where(slot_hit.T, gate_weights.reshape(-1)[:, None], jnp.float32(0.0))
    gate_at = jnp.sum(gate_at.reshape(tok_dev, TOPK, experts * capacity), axis=1)
    expert_sum = jnp.dot(
        gate_at,
        summed_rows.astype(jnp.float32),
        precision=lax.Precision.HIGHEST,
        preferred_element_type=jnp.float32,
    )
    return (residual + expert_sum).astype(jnp.bfloat16)


def solution(mesh):
    placed = (
        P(WN, None),
        P(WN, None),
        P(WN, None),
        P("wide", NARROW, None),
        P("wide", None),
        P("wide", None),
        P("wide", None, None),
        P(),
        P(),
        P(),
        P(WN, None),
        P(WN, None),
        P(WN, None, None),
        P(WN, None, None),
    )
    mesh = Mesh(mesh.devices.reshape(mesh.shape["wide"], -1, 2), ("wide", "y", "core"))
    return jax.shard_map(
        shards, mesh=mesh, in_specs=placed, out_specs=P(WN, None), check_vma=False
    )
```

```python
import functools

import jax
import jax.numpy as jnp
from jax import lax
from jax.experimental import pallas as pl
from jax.experimental.pallas import tpu as pltpu
from jax.sharding import Mesh
from jax.sharding import PartitionSpec as P

QH = 16
KVH = 4
HD = 128
TOPK = 6
PAGE_CAP = 2
NARROW = ("y", "core")
CHIPS = ("wide", "y")
WN = ("wide", "y", "core")


norm_eps = 1e-06
block_limit = 512
BQ = 128
BK = 128
LANES = 128


def rank_among_equal(values):
    length = values.shape[0]
    order = jnp.arange(length, dtype=jnp.int32)
    earlier = (values[None, :] == values[:, None]) & (order[None, :] < order[:, None])
    return jnp.sum(earlier.astype(jnp.int32), axis=1)


def block_scores(q_block, keys):
    return jnp.einsum("bhd,kd->hbk", q_block, keys, preferred_element_type=jnp.float32) * HD ** (
        -0.5
    )


def fresh_scores(start_row, q_heads, key_new, seg_all, block_len):
    q_block = lax.dynamic_slice_in_dim(q_heads, start_row, block_len, 0)
    seg_block = lax.dynamic_slice_in_dim(seg_all, start_row, block_len, 0)
    row_pos = start_row + jnp.arange(block_len, dtype=jnp.int32)
    positions = jnp.arange(seg_all.shape[0], dtype=jnp.int32)
    visible = (seg_block[:, None] == seg_all[None, :]) & (positions[None, :] <= row_pos[:, None])
    scores = jnp.where(visible[None], block_scores(q_block, key_new), -jnp.inf)
    return (q_block, seg_block, scores)


def attend_masked(
    start_row,
    q_heads,
    key_new,
    value_new,
    key_cached,
    value_cached,
    seg_all,
    lengths,
    cache_max,
    block_len,
):
    q_block, seg_block, fresh = fresh_scores(start_row, q_heads, key_new, seg_all, block_len)
    key_req = jnp.arange(key_cached.shape[0], dtype=jnp.int32) // cache_max
    key_pos = jnp.arange(key_cached.shape[0], dtype=jnp.int32) % cache_max
    visible = (seg_block[:, None] == key_req[None, :]) & (
        key_pos[None, :] < lengths[key_req][None, :]
    )
    older = jnp.where(visible[None], block_scores(q_block, key_cached), -jnp.inf)
    row_max = jnp.maximum(jnp.max(fresh, axis=-1), jnp.max(older, axis=-1))
    fresh_exp = jnp.exp(fresh - row_max[..., None])
    older_exp = jnp.exp(older - row_max[..., None])
    row_total = jnp.sum(fresh_exp, axis=-1) + jnp.sum(older_exp, axis=-1)
    fresh_w = (fresh_exp / row_total[..., None]).astype(jnp.bfloat16)
    older_w = (older_exp / row_total[..., None]).astype(jnp.bfloat16)
    attended = jnp.einsum("hbk,kd->bhd", fresh_w, value_new, preferred_element_type=jnp.float32)
    attended = attended + jnp.einsum(
        "hbk,kd->bhd", older_w, value_cached, preferred_element_type=jnp.float32
    )
    return attended.astype(jnp.bfloat16).reshape(block_len, -1)


def slot_attention(q_rows, kv_new, kv_cached, seg_all, lengths, cache_max):
    tokens = q_rows.shape[0]
    slots = lengths.shape[0]
    scale = HD ** (-0.5)
    n_q = tokens // BQ
    new_steps = (cache_max + BQ) // BK
    steps = new_steps + slots
    seg_start = jnp.sum(
        (seg_all[None, :] < jnp.arange(slots, dtype=jnp.int32)[:, None]).astype(jnp.int32), axis=1
    )
    firsts = seg_all[::BQ]
    lasts = seg_all[BQ - 1 :: BQ]
    kb_hi = (jnp.arange(n_q, dtype=jnp.int32) * BQ + BQ - 1) // BK
    kb_lo = jnp.maximum(seg_start[firsts] // BK, kb_hi - (new_steps - 1))
    n_new = kb_hi - kb_lo + 1
    n_old = lasts - firsts + 1
    t = jnp.arange(steps, dtype=jnp.int32)[None, :]
    new_idx = (kb_lo[:, None] + jnp.minimum(t, n_new[:, None] - 1)).reshape(-1)
    old_idx = (firsts[:, None] + jnp.clip(t - n_new[:, None], 0, n_old[:, None] - 1)).reshape(-1)
    counts = jnp.stack([n_new, n_old], axis=1).reshape(-1)
    q2 = q_rows.reshape(n_q, BQ, 2, HD).transpose(0, 2, 1, 3).reshape(n_q, 2 * BQ, HD)
    seg_q = jnp.broadcast_to(seg_all.reshape(n_q, 1, BQ, 1), (n_q, 2, BQ, LANES)).reshape(n_q, 2 * BQ, LANES)
    seg_k = jnp.broadcast_to(seg_all.reshape(tokens // BK, 1, BK), (tokens // BK, 8, BK))
    cached = kv_cached.reshape(slots, cache_max, 2 * HD)

    def kernel(new_sm, old_sm, cnt_sm, len_sm, q_ref, segq_ref, kn_ref, vn_ref, segk_ref, kc_ref, vc_ref, o_ref,
               m_ref, l_ref, acc_ref):
        b = pl.program_id(0)
        step = pl.program_id(1)
        nn = cnt_sm[2 * b]
        no = cnt_sm[2 * b + 1]

        @pl.when(step == 0)
        def _():
            m_ref[...] = jnp.full(m_ref.shape, -1e30, jnp.float32)
            l_ref[...] = jnp.zeros(l_ref.shape, jnp.float32)
            acc_ref[...] = jnp.zeros(acc_ref.shape, jnp.float32)

        def widen(x, width):
            return x if width == LANES else jnp.concatenate([x] * (width // LANES), axis=1)

        def visit(s, v):
            m = m_ref[...]
            m_new = jnp.maximum(m, jnp.max(s, axis=1, keepdims=True))
            alpha = jnp.exp(m - m_new)
            p = jnp.exp(s - widen(m_new, s.shape[1]))
            l_ref[...] = l_ref[...] * alpha + jnp.sum(p, axis=1, keepdims=True)
            acc_ref[...] = acc_ref[...] * alpha + jnp.dot(
                p.astype(jnp.bfloat16), v, preferred_element_type=jnp.float32)
            m_ref[...] = m_new

        q = q_ref[0]
        sq = segq_ref[0]

        @pl.when(step < nn)
        def _():
            kb = new_sm[b * steps + step]
            s = lax.dot_general(q, kn_ref[...], (((1,), (1,)), ((), ())),
                                preferred_element_type=jnp.float32) * scale
            rows = lax.broadcasted_iota(jnp.int32, s.shape, 0)
            cols = lax.broadcasted_iota(jnp.int32, s.shape, 1)
            qpos = b * BQ + jnp.bitwise_and(rows, BQ - 1)
            vis = (sq == segk_ref[0][:1, :]) & (kb * BK + cols <= qpos)
            visit(jnp.where(vis, s, -jnp.inf), vn_ref[...])

        @pl.when((step >= nn) & (step < nn + no))
        def _():
            r = old_sm[b * steps + step]
            s = lax.dot_general(q, kc_ref[0], (((1,), (1,)), ((), ())),
                                preferred_element_type=jnp.float32) * scale
            cols = lax.broadcasted_iota(jnp.int32, s.shape, 1)
            vis = (widen(sq, s.shape[1]) == r) & (cols < len_sm[r])
            visit(jnp.where(vis, s, -jnp.inf), vc_ref[0])

        @pl.when(step == steps - 1)
        def _():
            o_ref[0] = (acc_ref[...] / l_ref[...]).astype(jnp.bfloat16)

    def at(table):
        return lambda b, t, new_sm, old_sm, cnt_sm, len_sm: table(b, t, new_sm, old_sm)

    grid_spec = pltpu.PrefetchScalarGridSpec(
        num_scalar_prefetch=4,
        grid=(n_q, steps),
        in_specs=[
            pl.BlockSpec((1, 2 * BQ, HD), lambda b, t2, *_: (b, 0, 0)),
            pl.BlockSpec((1, 2 * BQ, LANES), lambda b, t2, *_: (b, 0, 0)),
            pl.BlockSpec((BK, HD), at(lambda b, t, n, o: (n[b * steps + t], 0))),
            pl.BlockSpec((BK, HD), at(lambda b, t, n, o: (n[b * steps + t], 1))),
            pl.BlockSpec((1, 8, BK), at(lambda b, t, n, o: (n[b * steps + t], 0, 0))),
            pl.BlockSpec((1, cache_max, HD), at(lambda b, t, n, o: (o[b * steps + t], 0, 0))),
            pl.BlockSpec((1, cache_max, HD), at(lambda b, t, n, o: (o[b * steps + t], 0, 1))),
        ],
        out_specs=pl.BlockSpec((1, 2 * BQ, HD), lambda b, t2, *_: (b, 0, 0)),
        scratch_shapes=[
            pltpu.VMEM((2 * BQ, LANES), jnp.float32),
            pltpu.VMEM((2 * BQ, LANES), jnp.float32),
            pltpu.VMEM((2 * BQ, HD), jnp.float32),
        ],
    )
    out = pl.pallas_call(
        kernel,
        grid_spec=grid_spec,
        out_shape=jax.ShapeDtypeStruct((n_q, 2 * BQ, HD), jnp.bfloat16),
    )(new_idx, old_idx, counts, lengths, q2, seg_q, kv_new, kv_new, seg_k, cached, cached)
    return out.reshape(n_q, 2, BQ, HD).transpose(0, 2, 1, 3).reshape(tokens, 2 * HD)


def expert_apply(rows_in, expert_in, expert_out):
    dims_in = rows_in.shape
    flat = rows_in.reshape(-1, dims_in[-1])
    both = jnp.dot(flat, expert_in[0], preferred_element_type=jnp.float32)
    half_units = both.shape[1] // 2
    hidden = (jax.nn.silu(both[:, :half_units]) * both[:, half_units:]).astype(jnp.bfloat16)
    half_out = jnp.dot(hidden, expert_out[0], preferred_element_type=jnp.float32)
    return half_out.reshape(dims_in)


def shards(
    tokens,
    queries,
    new_kv,
    page_pool,
    seg_ids,
    cache_len,
    page_table,
    moves,
    out_weight,
    norm_gain,
    expert_ids,
    gate_weights,
    expert_in,
    expert_out,
):
    n_wide = lax.axis_size("wide")
    n_narrow = lax.axis_size("y") * lax.axis_size("core")
    my_group = lax.axis_index("wide")
    tok_dev, width = tokens.shape
    group_tok = tok_dev * n_narrow
    requests = moves.shape[0]
    page_rows = page_pool.shape[1]
    kv_feat = page_pool.shape[2]
    pages_each = page_pool.shape[0] // requests
    heads_here = QH // n_narrow
    group_size = QH // KVH
    ranks = rank_among_equal(moves)
    offsets = jnp.arange(n_wide, dtype=jnp.int32)
    places = jnp.arange(PAGE_CAP, dtype=jnp.int32)
    slot_hits = (moves[None, None, :] == offsets[:, None, None]) & (
        ranks[None, None, :] == places[None, :, None]
    )
    picked = jnp.sum(slot_hits.astype(jnp.int32) * jnp.arange(requests, dtype=jnp.int32), axis=2)
    by_dest = (offsets - my_group) % n_wide
    picked = picked[by_dest]
    blocks = page_pool.reshape(requests, pages_each * page_rows, kv_feat)
    outgoing = jnp.take(blocks, picked.reshape(-1), axis=0).reshape(
        n_wide, PAGE_CAP, pages_each * page_rows, kv_feat
    )
    arrived = lax.all_to_all(outgoing, "wide", split_axis=0, concat_axis=0, tiled=True)
    sources = (my_group - moves) % n_wide
    first_page = (sources * PAGE_CAP + ranks) * pages_each
    page_index = (first_page[:, None] + page_table[0]).reshape(-1)
    arrived = arrived.reshape(n_wide * PAGE_CAP * pages_each, page_rows, kv_feat)
    cached = jnp.take(arrived, page_index, axis=0)
    kv_of_dest = jnp.arange(n_narrow, dtype=jnp.int32) * heads_here // group_size
    q_send = queries.reshape(1, tok_dev, n_narrow, heads_here * HD)
    kv_send = jnp.take(new_kv.reshape(tok_dev, KVH, 2 * HD), kv_of_dest, axis=1).reshape(
        1, tok_dev, n_narrow, 2 * HD
    )
    cache_send = jnp.take(
        cached.reshape(requests * pages_each, page_rows, KVH, 2 * HD), kv_of_dest, axis=2
    )
    q_heads, kv_heads, cache_heads = (
        lax.all_to_all(q_send, NARROW, split_axis=2, concat_axis=1, tiled=True),
        lax.all_to_all(kv_send, NARROW, split_axis=2, concat_axis=1, tiled=True),
        lax.all_to_all(cache_send, NARROW, split_axis=2, concat_axis=1, tiled=True),
    )
    q_heads = q_heads.reshape(group_tok, heads_here, HD)
    kv_heads = kv_heads.reshape(group_tok, 2 * HD)
    cache_max = pages_each * page_rows * n_narrow
    cache_heads = cache_heads.reshape(requests * cache_max, 2 * HD)
    key_new = kv_heads[:, :HD]
    value_new = kv_heads[:, HD:]
    key_cached = cache_heads[:, :HD]
    value_cached = cache_heads[:, HD:]
    seg_all = seg_ids[0]
    lengths = cache_len[0]
    attended = slot_attention(
        q_heads.reshape(group_tok, heads_here * HD), kv_heads, cache_heads, seg_all, lengths, cache_max
    ).reshape(n_narrow, tok_dev, heads_here * HD)
    back_home = lax.all_to_all(attended, NARROW, split_axis=0, concat_axis=2, tiled=True)
    mixed = back_home.reshape(tok_dev, QH * HD)
    residual = tokens.astype(jnp.float32) + jnp.dot(
        mixed, out_weight, preferred_element_type=jnp.float32
    )
    scale_row = lax.rsqrt(jnp.mean(residual * residual, axis=-1, keepdims=True) + norm_eps)
    normed = (residual * scale_row * norm_gain).astype(jnp.bfloat16)
    experts = n_wide * n_narrow // 2
    capacity = tok_dev * TOPK * 4 // (3 * experts)
    flat_ids = expert_ids.reshape(-1)
    onehot = (flat_ids[:, None] == jnp.arange(experts, dtype=jnp.int32)[None, :]).astype(jnp.int32)
    pairs = flat_ids.shape[0]
    earlier = (
        lax.broadcasted_iota(jnp.int32, (pairs, pairs), 1) < lax.broadcasted_iota(jnp.int32, (pairs, pairs), 0)
    ).astype(jnp.bfloat16)
    before = jnp.dot(earlier, onehot.astype(jnp.bfloat16), preferred_element_type=jnp.float32).astype(jnp.int32)
    slot_place = jnp.sum(before * onehot, axis=1)
    slot_of = flat_ids * capacity + slot_place
    slot_hit = slot_of[None, :] == jnp.arange(experts * capacity, dtype=jnp.int32)[:, None]
    pick = jnp.any(slot_hit.reshape(experts * capacity, tok_dev, TOPK), axis=2).astype(jnp.bfloat16)
    outgoing_rows = jnp.dot(pick, normed, preferred_element_type=jnp.float32).astype(jnp.bfloat16)
    outgoing_rows = outgoing_rows.reshape(experts, capacity, width)
    at_chip = lax.all_to_all(outgoing_rows, CHIPS, split_axis=0, concat_axis=0, tiled=True)
    swap = [(0, 1), (1, 0)]
    partner_rows = lax.ppermute(at_chip, "core", perm=swap)
    own_half = expert_apply(at_chip, expert_in, expert_out)
    own_half, partner_rows = lax.optimization_barrier((own_half, partner_rows))
    partner_half = expert_apply(partner_rows, expert_in, expert_out)
    other_half = lax.ppermute(partner_half.astype(jnp.bfloat16), "core", perm=swap)
    summed = (own_half + other_half.astype(jnp.float32)).astype(jnp.bfloat16)
    returned = lax.all_to_all(summed, CHIPS, split_axis=0, concat_axis=0, tiled=True)
    summed_rows = returned.reshape(experts * capacity, width)
    gate_at = jnp.where(slot_hit.T, gate_weights.reshape(-1)[:, None], jnp.float32(0.0))
    gate_at = jnp.sum(gate_at.reshape(tok_dev, TOPK, experts * capacity), axis=1)
    expert_sum = jnp.dot(
        gate_at,
        summed_rows.astype(jnp.float32),
        precision=lax.Precision.HIGHEST,
        preferred_element_type=jnp.float32,
    )
    return (residual + expert_sum).astype(jnp.bfloat16)


def solution(mesh):
    placed = (
        P(WN, None),
        P(WN, None),
        P(WN, None),
        P("wide", NARROW, None),
        P("wide", None),
        P("wide", None),
        P("wide", None, None),
        P(),
        P(),
        P(),
        P(WN, None),
        P(WN, None),
        P(WN, None, None),
        P(WN, None, None),
    )
    mesh = Mesh(mesh.devices.reshape(mesh.shape["wide"], -1, 2), ("wide", "y", "core"))
    return jax.shard_map(
        shards, mesh=mesh, in_specs=placed, out_specs=P(WN, None), check_vma=False
    )
```
